256 devices in a mesh: pipe: 32 (over x, z), dp: 8 (over y, core).
Axes of the slice: x: 4, y: 4, z: 8, core: 2. Of those that a mesh axis runs over, the one named last changes fastest.
Arguments:
- query_acts: bfloat16 [32, 8, 256, 3584], P('pipe', 'dp'), may hold values from -5.5 to 5.5
- key_acts: bfloat16 [32, 8, 256, 3584], P('pipe', 'dp'), may hold values from -5.5 to 5.5
- layer_inputs: bfloat16 [32, 8, 256, 3584], P('pipe', 'dp'), may hold values from -6 to 6
- grad_out: bfloat16 [8, 256, 3584], P('dp'), may hold values from -6 to 6
- norm_gains: float32 [32, 3584], P('pipe'), may hold values from -0.4 to 0.4
- window_flags: int32 [32], replicated, may hold values from 0 to 1
Outputs:
- grad_inputs: bfloat16 [32, 8, 256, 3584], P('pipe', 'dp')
- grad_queries: bfloat16 [32, 8, 256, 3584], P('pipe', 'dp')
- grad_keys: bfloat16 [32, 8, 256, 3584], P('pipe', 'dp')
- grad_gains: float32 [32, 3584], P('pipe', 'dp')
The draws below stay inside these ranges and needn't reach their ends.
All inputs are finite; a program needn't handle non-finite values.
Results may differ from the reference program's by a relative error of at most 0.012.
The reference program's roundings to bfloat16 on the way count: a program that leaves them out, or rounds other values in their place, can miss the bound.
Values may be sent and summed in bfloat16 or wider, within the bound.
No kernel may reach another device: no remote copies, remote signals or barrier semaphores. Data moves between devices by JAX's collectives and lax.ppermute only.
A program may use at most 64 MiB of HBM per device.

```python
import jax
import jax.numpy as jnp
from jax import lax

HEADS = 32
HEAD_DIM = 112
WIDTH = 3584
SEQ = 256
WINDOW = 32
LAYERS = 32
SEQS = 8


def drawn_pair(key):
    full_shape = (LAYERS, SEQS, SEQ, HEADS * HEAD_DIM)
    query_base = jnp.clip(jax.random.normal(jax.random.fold_in(key, 7), full_shape, jnp.float32), -5.5, 5.5)
    key_base = jnp.clip(jax.random.normal(jax.random.fold_in(key, 8), full_shape, jnp.float32), -5.5, 5.5)
    return (query_base, key_base)


def draw_query_acts(key, part):
    return drawn_pair(key)[0].astype(jnp.bfloat16)


def draw_key_acts(key, part):
    return drawn_pair(key)[1].astype(jnp.bfloat16)


def draw_norm_gains(key, part):
    gain_shape = (LAYERS, HEADS * HEAD_DIM)
    signs = (2 * jax.random.randint(jax.random.fold_in(key, 31), gain_shape, 0, 2, jnp.int32) - 1).astype(jnp.float32)
    magnitude = jax.random.uniform(jax.random.fold_in(key, 32), gain_shape, jnp.float32, 0.1, 0.4)
    return (signs * magnitude).astype(jnp.float32)


def draw_window_flags(key, part):
    scores = jax.random.randint(jax.random.fold_in(key, 21), (HEADS,), 0, 1000000, jnp.int32)
    distinct = scores * HEADS + jnp.arange(HEADS, dtype=jnp.int32)
    order = jnp.argsort(distinct, stable=True)
    ranks = jnp.zeros((HEADS,), jnp.int32).at[order].set(jnp.arange(HEADS, dtype=jnp.int32))
    return (ranks < HEADS // 2).astype(jnp.int32)


def steps_of(key, extent, split, low, top_value):
    gain = 1.0
    for axis_at, parts in split:
        draws = jax.random.uniform(jax.random.fold_in(jax.random.fold_in(key, 6), axis_at), (parts,), jnp.float32, low / len(split), top_value / len(split))
        gain = gain * jnp.repeat(jnp.exp(draws), extent[axis_at] // parts).reshape((-1,) + (1,) * (len(extent) - 1 - axis_at))
    return gain


def scatter_about(key, extent, width, most, split=(), kind=jnp.bfloat16):
    gain = steps_of(key, extent, split, -0.22, 0.18) if split else 1.0
    array = jax.random.normal(key, extent, jnp.float32) * width * gain
    return jnp.minimum(jnp.maximum(array, -most), most).astype(kind)


def setup_inputs(seed: int = 0) -> dict:
    key_of = jax.random.split(jax.random.key(seed), 7)
    return {
        "query_acts": draw_query_acts(jax.random.fold_in(key_of[6], 71), 0),
        "key_acts": draw_key_acts(jax.random.fold_in(key_of[6], 71), 0),
        "layer_inputs": scatter_about(key_of[2], (LAYERS, SEQS, SEQ, WIDTH), 1.0, 6.0, ((0, 32), (1, 8))),
        "grad_out": scatter_about(key_of[3], (SEQS, SEQ, WIDTH), 1.0, 6.0, ((0, 8),)),
        "norm_gains": draw_norm_gains(jax.random.fold_in(key_of[6], 71), 0),
        "window_flags": draw_window_flags(jax.random.fold_in(key_of[6], 71), 0),
    }


EPSILON = 1e-05
NEGATIVE = -1e+30

def head_slopes():
    numbers = jnp.arange(HEADS, dtype=jnp.float32) + 1.0
    return jnp.exp2(-numbers * 8.0 / HEADS)

def allowed_mask(window_flags):
    places = jnp.arange(SEQ, dtype=jnp.int32)
    distance = places[:, None] - places[None, :]
    causal = distance >= 0
    inside = distance < WINDOW
    allowed = causal[None, :, :] & ((window_flags[:, None, None] == 0) | inside[None, :, :])
    return (allowed, distance.astype(jnp.float32))

def softmax_rows(logits, allowed):
    masked = jnp.where(allowed, logits, NEGATIVE)
    row_top = lax.optimization_barrier(jnp.max(masked, axis=-1, keepdims=True))
    log_total = row_top + jnp.log(lax.optimization_barrier(jnp.sum(jnp.exp(masked - row_top), axis=-1, keepdims=True)))
    return jnp.where(allowed, jnp.exp(masked - log_total), 0.0)

def layer_backward(incoming, input_seq, query_seq, key_seq, gain_row, window_flags, slopes):
    input_float = input_seq.astype(jnp.float32)
    inverse = lax.rsqrt(lax.optimization_barrier(jnp.mean(input_float * input_float, axis=-1, keepdims=True)) + EPSILON)
    normed = input_float * inverse
    values = (normed * gain_row).astype(jnp.bfloat16)
    score_scale = HEAD_DIM ** (-0.5)
    allowed, distance = allowed_mask(window_flags)
    query_heads = query_seq.astype(jnp.float32).reshape(SEQ, HEADS, HEAD_DIM)
    key_heads = key_seq.astype(jnp.float32).reshape(SEQ, HEADS, HEAD_DIM)
    value_heads = values.astype(jnp.float32).reshape(SEQ, HEADS, HEAD_DIM)
    grad_heads = incoming.astype(jnp.float32).reshape(SEQ, HEADS, HEAD_DIM)
    logits = jnp.einsum('ihd,jhd->hij', query_heads, key_heads) * score_scale - slopes[:, None, None] * distance[None, :, :]
    weights = softmax_rows(logits, allowed)
    weights_low = lax.optimization_barrier(weights.astype(jnp.bfloat16)).astype(jnp.float32)
    attended = jnp.einsum('hij,jhd->ihd', weights_low, value_heads)
    delta_rows = jnp.einsum('ihd,ihd->hi', grad_heads, attended)
    grad_weights = jnp.einsum('ihd,jhd->hij', grad_heads, value_heads)
    grad_logits = (weights * (grad_weights - delta_rows[:, :, None])).astype(jnp.bfloat16)
    grad_logits = lax.optimization_barrier(grad_logits).astype(jnp.float32)
    grad_query = (jnp.einsum('hij,jhd->ihd', grad_logits, key_heads) * score_scale).astype(jnp.bfloat16).reshape(SEQ, WIDTH)
    grad_key = (jnp.einsum('hij,ihd->jhd', grad_logits, query_heads) * score_scale).astype(jnp.bfloat16).reshape(SEQ, WIDTH)
    grad_value = jnp.einsum('hij,ihd->jhd', weights_low, grad_heads).reshape(SEQ, WIDTH)
    gain_part = lax.optimization_barrier(jnp.sum(grad_value * normed, axis=0))
    grad_normed = grad_value * gain_row
    grad_input = incoming.astype(jnp.float32) + inverse * (grad_normed - normed * lax.optimization_barrier(jnp.mean(grad_normed * normed, axis=-1, keepdims=True)))
    return (grad_input.astype(jnp.bfloat16), grad_query, grad_key, gain_part)

def reference(query_acts, key_acts, layer_inputs, grad_out, norm_gains, window_flags):
    slopes = head_slopes()
    per_sequence = jax.vmap(layer_backward, in_axes=(0, 0, 0, 0, None, None, None))

    def one_layer(incoming, layer_data):
        query_layer, key_layer, input_layer, gain_row = layer_data
        grad_input, grad_query, grad_key, gain_part = per_sequence(incoming, input_layer, query_layer, key_layer, gain_row, window_flags, slopes)
        return (grad_input, (grad_input, grad_query, grad_key, lax.optimization_barrier(jnp.sum(gain_part, axis=0))))
    final_grad, stacked = lax.scan(one_layer, grad_out, (query_acts, key_acts, layer_inputs, norm_gains), reverse=True)
    return (stacked[0], stacked[1], stacked[2], stacked[3])
```

```python
import jax
import jax.numpy as jnp
from jax import lax
from jax.sharding import PartitionSpec as P

GROUPS = 8
WINDOW = 32


EPSILON = 1e-05
NEGATIVE = -1e30


def passed_along(value, axis, steps):
    count = lax.axis_size(axis)
    leading, last = (max(0, -steps), min(count, count - steps))
    return lax.ppermute(value, axis, [(source, source + steps) for source in range(leading, last)])


def rows_of(source, first_index, row_count):
    return lax.dynamic_slice_in_dim(source, first_index, row_count, 0)


def write_rows(buffer, first_index, new_rows):
    return lax.dynamic_update_slice_in_dim(buffer, new_rows, first_index, 0)


def on_device(query_acts, key_acts, layer_inputs, grad_out, norm_gains, window_flags):
    section_count = lax.axis_size("pipe")
    section_index = lax.axis_index("pipe")
    seq_rows = query_acts.shape[2]
    feature_count = query_acts.shape[3]
    head_count = window_flags.shape[0]
    head_size = feature_count // head_count
    score_scale = head_size ** (-0.5)
    slopes = jnp.exp2(-(jnp.arange(head_count, dtype=jnp.float32) + 1.0) * 8.0 / head_count)
    open_heads = (window_flags == 0)[:, None, None]
    query_rows = query_acts[0, 0]
    key_rows = key_acts[0, 0]
    from_loss = grad_out[0]
    input_rows = layer_inputs[0, 0].astype(jnp.float32)
    inverse = lax.rsqrt(jnp.mean(input_rows * input_rows, axis=-1, keepdims=True) + EPSILON)
    normed = input_rows * inverse
    gain_row = norm_gains[0]
    value_rows = (normed * gain_row).astype(jnp.bfloat16)
    places = jnp.arange(seq_rows, dtype=jnp.int32)
    all_queries = query_rows.reshape(seq_rows, head_count, head_size)
    all_keys = key_rows.reshape(seq_rows, head_count, head_size)
    all_values = value_rows.reshape(seq_rows, head_count, head_size)

    distance = places[:, None] - places[None, :]
    allowed = (distance >= 0)[None, :, :] & (open_heads | (distance < WINDOW)[None, :, :])
    logits = (
        jnp.einsum("ihd,jhd->hij", all_queries, all_keys, preferred_element_type=jnp.float32)
        * score_scale
    )
    logits = logits - slopes[:, None, None] * distance.astype(jnp.float32)[None, :, :]
    masked = jnp.where(allowed, logits, NEGATIVE)
    row_top = jnp.max(masked, axis=-1, keepdims=True)
    log_total = row_top + jnp.log(jnp.sum(jnp.exp(masked - row_top), axis=-1, keepdims=True))
    weights = jnp.where(allowed, jnp.exp(masked - log_total), 0.0)
    weights_low = weights.astype(jnp.bfloat16)
    attended = jnp.einsum(
        "hij,jhd->ihd", weights_low, all_values, preferred_element_type=jnp.float32
    )

    unit_count = GROUPS
    rows_here = seq_rows // unit_count
    column_blocks = jnp.pad(weights_low, ((0, 0), (0, rows_here), (0, 0)))
    column_blocks = column_blocks.reshape(
        head_count, seq_rows + rows_here, unit_count, rows_here
    ).transpose(2, 0, 1, 3)

    def one_turn(turn_index, carried):
        message, grad_buffer, input_grads = carried
        unit_index = turn_index - (section_count - 1 - section_index)
        active = (unit_index >= 0) & (unit_index < unit_count)
        chosen = jnp.clip(unit_count - 1 - unit_index, 0, unit_count - 1)
        first_row = chosen * rows_here
        slot = jnp.where(active, first_row, seq_rows)
        incoming = jnp.where(
            section_index == section_count - 1, rows_of(from_loss, first_row, rows_here), message
        )
        incoming = jnp.where(active, incoming, jnp.zeros_like(incoming))
        grad_buffer = write_rows(grad_buffer, slot, incoming)
        block = column_blocks[chosen]
        grad_value = jnp.einsum(
            "hij,ihd->jhd",
            block,
            grad_buffer.reshape(seq_rows + rows_here, head_count, head_size),
            preferred_element_type=jnp.float32,
        ).reshape(rows_here, feature_count)
        own_normed = rows_of(normed, first_row, rows_here)
        own_inverse = rows_of(inverse, first_row, rows_here)
        grad_normed = grad_value * gain_row
        grad_input = incoming.astype(jnp.float32) + own_inverse * (
            grad_normed - own_normed * jnp.mean(grad_normed * own_normed, axis=-1, keepdims=True)
        )
        grad_input = grad_input.astype(jnp.bfloat16)
        input_grads = write_rows(input_grads, slot, grad_input)
        return (passed_along(grad_input, "pipe", -1), grad_buffer, input_grads)

    initial = (
        jnp.zeros((rows_here, feature_count), jnp.bfloat16),
        jnp.zeros((seq_rows + rows_here, feature_count), jnp.bfloat16),
        jnp.zeros((seq_rows + rows_here, feature_count), jnp.bfloat16),
    )
    _, grad_buffer, input_grads = lax.fori_loop(
        0, unit_count + section_count - 1, one_turn, initial
    )
    grad_rows = grad_buffer[:seq_rows]
    grad_heads = grad_rows.reshape(seq_rows, head_count, head_size)

    delta_rows = jnp.einsum("ihd,ihd->hi", grad_heads.astype(jnp.float32), attended)
    grad_weights = jnp.einsum(
        "ihd,jhd->hij", grad_heads, all_values, preferred_element_type=jnp.float32
    )
    grad_logits = (weights * (grad_weights - delta_rows[:, :, None])).astype(jnp.bfloat16)
    grad_query = (
        jnp.einsum("hij,jhd->ihd", grad_logits, all_keys, preferred_element_type=jnp.float32)
        * score_scale
    )
    grad_query = grad_query.astype(jnp.bfloat16).reshape(seq_rows, feature_count)
    grad_key = (
        jnp.einsum("hij,ihd->jhd", grad_logits, all_queries, preferred_element_type=jnp.float32)
        * score_scale
    )
    grad_key = grad_key.astype(jnp.bfloat16).reshape(seq_rows, feature_count)
    grad_value = jnp.einsum(
        "hij,ihd->jhd", weights_low, grad_heads, preferred_element_type=jnp.float32
    ).reshape(seq_rows, feature_count)
    gain_sum = jnp.sum(grad_value * normed, axis=0)

    grad_queries = grad_query.reshape(1, 1, seq_rows, feature_count)
    grad_keys = grad_key.reshape(1, 1, seq_rows, feature_count)
    grad_inputs = input_grads[:seq_rows].reshape(1, 1, seq_rows, feature_count)
    grad_gains = lax.psum_scatter(gain_sum[None, :], "dp", scatter_dimension=1, tiled=True)
    return (grad_inputs, grad_queries, grad_keys, grad_gains)


def solution(mesh):
    return jax.shard_map(
        on_device,
        mesh=mesh,
        in_specs=(
            P("pipe", "dp", None, None),
            P("pipe", "dp", None, None),
            P("pipe", "dp", None, None),
            P("dp", None, None),
            P("pipe", None),
            P(),
        ),
        out_specs=(
            P("pipe", "dp", None, None),
            P("pipe", "dp", None, None),
            P("pipe", "dp", None, None),
            P("pipe", "dp"),
        ),
        check_vma=False,
    )
```

```python
import jax
import jax.numpy as jnp
from jax import lax
from jax.sharding import PartitionSpec as P

GROUPS = 8
WINDOW = 32


EPSILON = 1e-05
NEGATIVE = -1e30


def passed_along(value, axis, steps):
    count = lax.axis_size(axis)
    leading, last = (max(0, -steps), min(count, count - steps))
    return lax.ppermute(value, axis, [(source, source + steps) for source in range(leading, last)])


def rows_of(source, first_index, row_count):
    return lax.dynamic_slice_in_dim(source, first_index, row_count, 0)


def write_rows(buffer, first_index, new_rows):
    return lax.dynamic_update_slice_in_dim(buffer, new_rows, first_index, 0)


def on_device(query_acts, key_acts, layer_inputs, grad_out, norm_gains, window_flags):
    section_count = lax.axis_size("pipe")
    section_index = lax.axis_index("pipe")
    seq_rows = query_acts.shape[2]
    feature_count = query_acts.shape[3]
    head_count = window_flags.shape[0]
    head_size = feature_count // head_count
    score_scale = head_size ** (-0.5)
    slopes = jnp.exp2(-(jnp.arange(head_count, dtype=jnp.float32) + 1.0) * 8.0 / head_count)
    open_heads = (window_flags == 0)[:, None, None]
    query_rows = query_acts[0, 0]
    key_rows = key_acts[0, 0]
    from_loss = grad_out[0]
    input_rows = layer_inputs[0, 0].astype(jnp.float32)
    inverse = lax.rsqrt(jnp.mean(input_rows * input_rows, axis=-1, keepdims=True) + EPSILON)
    normed = input_rows * inverse
    gain_row = norm_gains[0]
    value_rows = (normed * gain_row).astype(jnp.bfloat16)
    places = jnp.arange(seq_rows, dtype=jnp.int32)
    all_queries = query_rows.reshape(seq_rows, head_count, head_size)
    all_keys = key_rows.reshape(seq_rows, head_count, head_size)
    all_values = value_rows.reshape(seq_rows, head_count, head_size)

    distance = places[:, None] - places[None, :]
    allowed = (distance >= 0)[None, :, :] & (open_heads | (distance < WINDOW)[None, :, :])
    logits = (
        jnp.einsum("ihd,jhd->hij", all_queries, all_keys, preferred_element_type=jnp.float32)
        * score_scale
    )
    logits = logits - slopes[:, None, None] * distance.astype(jnp.float32)[None, :, :]
    masked = jnp.where(allowed, logits, NEGATIVE)
    row_top = jnp.max(masked, axis=-1, keepdims=True)
    log_total = row_top + jnp.log(jnp.sum(jnp.exp(masked - row_top), axis=-1, keepdims=True))
    weights = jnp.where(allowed, jnp.exp(masked - log_total), 0.0)
    weights_low = weights.astype(jnp.bfloat16)
    attended = jnp.einsum(
        "hij,jhd->ihd", weights_low, all_values, preferred_element_type=jnp.float32
    )

    unit_count = GROUPS
    rows_here = seq_rows // unit_count
    column_blocks = jnp.pad(weights_low, ((0, 0), (0, rows_here), (0, 0)))
    column_blocks = column_blocks.reshape(
        head_count, seq_rows + rows_here, unit_count, rows_here
    ).transpose(2, 0, 1, 3)
    spare_rows = seq_rows + rows_here

    def one_turn(turn_index, carried):
        message, grad_buffer, input_grads = carried
        unit_index = turn_index - (section_count - 1 - section_index)
        active = (unit_index >= 0) & (unit_index < unit_count)
        chosen = jnp.clip(unit_count - 1 - unit_index, 0, unit_count - 1)
        first_row = chosen * rows_here
        slot = jnp.where(active, first_row, seq_rows)
        incoming = jnp.where(
            section_index == section_count - 1, rows_of(from_loss, first_row, rows_here), message
        )
        incoming = jnp.where(active, incoming, jnp.zeros_like(incoming))
        incoming_heads = incoming.reshape(rows_here, head_count, head_size).transpose(1, 0, 2)
        grad_buffer = lax.dynamic_update_slice_in_dim(grad_buffer, incoming_heads, slot, 1)
        block = column_blocks[chosen]
        grad_value = jnp.einsum(
            "hij,hid->jhd", block, grad_buffer, preferred_element_type=jnp.float32
        ).reshape(rows_here, feature_count)
        own_normed = rows_of(normed, first_row, rows_here)
        own_inverse = rows_of(inverse, first_row, rows_here)
        grad_normed = grad_value * gain_row
        grad_input = incoming.astype(jnp.float32) + own_inverse * (
            grad_normed - own_normed * jnp.mean(grad_normed * own_normed, axis=-1, keepdims=True)
        )
        grad_input = grad_input.astype(jnp.bfloat16)
        input_grads = write_rows(input_grads, slot, grad_input)
        return (passed_along(grad_input, "pipe", -1), grad_buffer, input_grads)

    initial = (
        jnp.zeros((rows_here, feature_count), jnp.bfloat16),
        jnp.zeros((head_count, spare_rows, head_size), jnp.bfloat16),
        jnp.zeros((spare_rows, feature_count), jnp.bfloat16),
    )
    _, grad_buffer, input_grads = lax.fori_loop(
        0, unit_count + section_count - 1, one_turn, initial
    )
    grad_heads = grad_buffer[:, :seq_rows].transpose(1, 0, 2)

    delta_rows = jnp.einsum("ihd,ihd->hi", grad_heads.astype(jnp.float32), attended)
    grad_weights = jnp.einsum(
        "ihd,jhd->hij", grad_heads, all_values, preferred_element_type=jnp.float32
    )
    grad_logits = (weights * (grad_weights - delta_rows[:, :, None])).astype(jnp.bfloat16)
    grad_query = (
        jnp.einsum("hij,jhd->ihd", grad_logits, all_keys, preferred_element_type=jnp.float32)
        * score_scale
    )
    grad_query = grad_query.astype(jnp.bfloat16).reshape(seq_rows, feature_count)
    grad_key = (
        jnp.einsum("hij,ihd->jhd", grad_logits, all_queries, preferred_element_type=jnp.float32)
        * score_scale
    )
    grad_key = grad_key.astype(jnp.bfloat16).reshape(seq_rows, feature_count)
    grad_value = jnp.einsum(
        "hij,ihd->jhd", weights_low, grad_heads, preferred_element_type=jnp.float32
    ).reshape(seq_rows, feature_count)
    gain_sum = jnp.sum(grad_value * normed, axis=0)

    grad_queries = grad_query.reshape(1, 1, seq_rows, feature_count)
    grad_keys = grad_key.reshape(1, 1, seq_rows, feature_count)
    grad_inputs = input_grads[:seq_rows].reshape(1, 1, seq_rows, feature_count)
    group_count = lax.axis_size("dp")
    gain_parts = lax.all_to_all(
        gain_sum.reshape(group_count, feature_count // group_count), "dp", 0, 0, tiled=True
    )
    grad_gains = jnp.sum(gain_parts, axis=0, keepdims=True)
    return (grad_inputs, grad_queries, grad_keys, grad_gains)


def solution(mesh):
    return jax.shard_map(
        on_device,
        mesh=mesh,
        in_specs=(
            P("pipe", "dp", None, None),
            P("pipe", "dp", None, None),
            P("pipe", "dp", None, None),
            P("dp", None, None),
            P("pipe", None),
            P(),
        ),
        out_specs=(
            P("pipe", "dp", None, None),
            P("pipe", "dp", None, None),
            P("pipe", "dp", None, None),
            P("pipe", "dp"),
        ),
        check_vma=False,
    )
```

```python
import functools
import math

import jax
import jax.numpy as jnp
from jax import lax
from jax.experimental import pallas as pl
from jax.experimental.pallas import tpu as pltpu
from jax.sharding import PartitionSpec as P

GROUPS = 8
WINDOW = 32


EPSILON = 1e-05
NEGATIVE = -1e30


def passed_along(value, axis, steps):
    count = lax.axis_size(axis)
    leading, last = (max(0, -steps), min(count, count - steps))
    return lax.ppermute(value, axis, [(source, source + steps) for source in range(leading, last)])


def rows_of(source, first_index, row_count):
    return lax.dynamic_slice_in_dim(source, first_index, row_count, 0)


def write_rows(buffer, first_index, new_rows):
    return lax.dynamic_update_slice_in_dim(buffer, new_rows, first_index, 0)


def turn_kernel(
    flags_ref,
    w_ref, wd_ref, g_ref, msg_ref, loss_ref, normed_ref, inv_ref, gain_ref,
    out_ref, inc_ref,
    gn_s, acc_s,
    *, group_lanes, head_size, rows_here, groups, feature_count,
):
    g = pl.program_id(0)
    from_loss = flags_ref[1] == 1
    active = flags_ref[2] == 1

    @pl.when(g == 0)
    def _():
        inc = jnp.where(from_loss, loss_ref[...], msg_ref[...])
        inc = jnp.where(active, inc, jnp.zeros_like(inc))
        inc_ref[...] = inc
        acc_s[...] = jnp.zeros_like(acc_s)

    lanes = pl.ds(pl.multiple_of(g * group_lanes, 128), group_lanes)
    inc_g = inc_ref[:, lanes]
    stacked = jnp.dot(w_ref[0, 0], g_ref[...], preferred_element_type=jnp.float32)
    stacked = stacked + jnp.dot(wd_ref[0, 0], inc_g, preferred_element_type=jnp.float32)
    lane_head = lax.broadcasted_iota(jnp.int32, (rows_here, group_lanes), 1) // head_size
    value = jnp.zeros((rows_here, group_lanes), jnp.float32)
    for k in range(group_lanes // head_size):
        value = value + jnp.where(
            lane_head == k, stacked[k * rows_here:(k + 1) * rows_here, :], 0.0
        )
    grad_normed = value * gain_ref[:, lanes]
    gn_s[g] = grad_normed
    acc_s[...] += jnp.sum(grad_normed * normed_ref[:, lanes], axis=1, keepdims=True)

    @pl.when(g == groups - 1)
    def _():
        mean = acc_s[...] * (1.0 / feature_count)
        inv = inv_ref[...]
        for k in range(groups):
            cols = slice(k * group_lanes, (k + 1) * group_lanes)
            out_ref[:, cols] = (
                inc_ref[:, cols].astype(jnp.float32)
                + inv * (gn_s[k] - normed_ref[:, cols] * mean)
            ).astype(out_ref.dtype)


def turn_call(flags, w_blocks, w_diag, grad_buffer, message, from_loss, normed, inverse, gain,
              *, head_size, rows_here):
    unit_count, groups, stack_rows, spare_rows = w_blocks.shape
    feature_count = grad_buffer.shape[1]
    group_lanes = feature_count // groups
    kernel = functools.partial(
        turn_kernel, group_lanes=group_lanes, head_size=head_size, rows_here=rows_here,
        groups=groups, feature_count=feature_count,
    )
    grid_spec = pltpu.PrefetchScalarGridSpec(
        num_scalar_prefetch=1,
        grid=(groups,),
        in_specs=[
            pl.BlockSpec((1, 1, stack_rows, spare_rows), lambda g, f: (f[0], g, 0, 0)),
            pl.BlockSpec((1, 1, stack_rows, rows_here), lambda g, f: (f[0], g, 0, 0)),
            pl.BlockSpec((spare_rows, group_lanes), lambda g, f: (0, g)),
            pl.BlockSpec((rows_here, feature_count), lambda g, f: (0, 0)),
            pl.BlockSpec((rows_here, feature_count), lambda g, f: (f[0], 0)),
            pl.BlockSpec((rows_here, feature_count), lambda g, f: (f[0], 0)),
            pl.BlockSpec((rows_here, 1), lambda g, f: (f[0], 0)),
            pl.BlockSpec((1, feature_count), lambda g, f: (0, 0)),
        ],
        out_specs=[
            pl.BlockSpec((rows_here, feature_count), lambda g, f: (0, 0)),
            pl.BlockSpec((rows_here, feature_count), lambda g, f: (0, 0)),
        ],
        scratch_shapes=[
            pltpu.VMEM((groups, rows_here, group_lanes), jnp.float32),
            pltpu.VMEM((rows_here, 1), jnp.float32),
        ],
    )
    return pl.pallas_call(
        kernel,
        grid_spec=grid_spec,
        out_shape=[
            jax.ShapeDtypeStruct((rows_here, feature_count), jnp.bfloat16),
            jax.ShapeDtypeStruct((rows_here, feature_count), jnp.bfloat16),
        ],
        compiler_params=pltpu.CompilerParams(dimension_semantics=("arbitrary",)),
    )(flags, w_blocks, w_diag, grad_buffer, message, from_loss, normed, inverse, gain)


def on_device(query_acts, key_acts, layer_inputs, grad_out, norm_gains, window_flags):
    section_count = lax.axis_size("pipe")
    section_index = lax.axis_index("pipe")
    seq_rows = query_acts.shape[2]
    feature_count = query_acts.shape[3]
    head_count = window_flags.shape[0]
    head_size = feature_count // head_count
    score_scale = head_size ** (-0.5)
    slopes = jnp.exp2(-(jnp.arange(head_count, dtype=jnp.float32) + 1.0) * 8.0 / head_count)
    open_heads = (window_flags == 0)[:, None, None]
    query_rows = query_acts[0, 0]
    key_rows = key_acts[0, 0]
    from_loss = grad_out[0]
    input_rows = layer_inputs[0, 0].astype(jnp.float32)
    inverse = lax.rsqrt(jnp.mean(input_rows * input_rows, axis=-1, keepdims=True) + EPSILON)
    normed = input_rows * inverse
    gain_row = norm_gains[0]
    value_rows = (normed * gain_row).astype(jnp.bfloat16)
    places = jnp.arange(seq_rows, dtype=jnp.int32)
    all_queries = query_rows.reshape(seq_rows, head_count, head_size)
    all_keys = key_rows.reshape(seq_rows, head_count, head_size)
    all_values = value_rows.reshape(seq_rows, head_count, head_size)

    distance = places[:, None] - places[None, :]
    allowed = (distance >= 0)[None, :, :] & (open_heads | (distance < WINDOW)[None, :, :])
    logits = (
        jnp.einsum("ihd,jhd->hij", all_queries, all_keys, preferred_element_type=jnp.float32)
        * score_scale
    )
    logits = logits - slopes[:, None, None] * distance.astype(jnp.float32)[None, :, :]
    masked = jnp.where(allowed, logits, NEGATIVE)
    row_top = jnp.max(masked, axis=-1, keepdims=True)
    log_total = row_top + jnp.log(jnp.sum(jnp.exp(masked - row_top), axis=-1, keepdims=True))
    weights = jnp.where(allowed, jnp.exp(masked - log_total), 0.0)
    weights_low = weights.astype(jnp.bfloat16)
    attended = jnp.einsum(
        "hij,jhd->ihd", weights_low, all_values, preferred_element_type=jnp.float32
    )

    unit_count = GROUPS
    rows_here = seq_rows // unit_count
    group_lanes = math.lcm(head_size, 128)
    groups = feature_count // group_lanes
    group_heads = group_lanes // head_size
    spare_rows = seq_rows + rows_here
    transposed = weights_low.transpose(0, 2, 1)
    w_blocks = jnp.pad(transposed, ((0, 0), (0, 0), (0, rows_here)))
    w_blocks = w_blocks.reshape(groups, group_heads, unit_count, rows_here, spare_rows)
    w_blocks = w_blocks.transpose(2, 0, 1, 3, 4).reshape(
        unit_count, groups, group_heads * rows_here, spare_rows
    )
    split = transposed.reshape(head_count, unit_count, rows_here, unit_count, rows_here)
    w_diag = jnp.stack([split[:, c, :, c, :] for c in range(unit_count)])
    w_diag = w_diag.reshape(unit_count, groups, group_heads * rows_here, rows_here)
    last_stage = (section_index == section_count - 1).astype(jnp.int32)
    gain_line = gain_row[None, :]

    def one_turn(turn_index, carried):
        message, grad_buffer, input_grads = carried
        unit_index = turn_index - (section_count - 1 - section_index)
        active = (unit_index >= 0) & (unit_index < unit_count)
        chosen = jnp.clip(unit_count - 1 - unit_index, 0, unit_count - 1)
        slot = jnp.where(active, chosen * rows_here, seq_rows)
        flags = jnp.stack([chosen, last_stage, active.astype(jnp.int32)])
        grad_input, incoming = turn_call(
            flags, w_blocks, w_diag, grad_buffer, message, from_loss, normed, inverse, gain_line,
            head_size=head_size, rows_here=rows_here,
        )
        grad_buffer = write_rows(grad_buffer, slot, incoming)
        input_grads = write_rows(input_grads, slot, grad_input)
        return (passed_along(grad_input, "pipe", -1), grad_buffer, input_grads)

    initial = (
        jnp.zeros((rows_here, feature_count), jnp.bfloat16),
        jnp.zeros((spare_rows, feature_count), jnp.bfloat16),
        jnp.zeros((spare_rows, feature_count), jnp.bfloat16),
    )
    _, grad_buffer, input_grads = lax.fori_loop(
        0, unit_count + section_count - 1, one_turn, initial
    )
    grad_heads = grad_buffer[:seq_rows].reshape(seq_rows, head_count, head_size)

    delta_rows = jnp.einsum("ihd,ihd->hi", grad_heads.astype(jnp.float32), attended)
    grad_weights = jnp.einsum(
        "ihd,jhd->hij", grad_heads, all_values, preferred_element_type=jnp.float32
    )
    grad_logits = (weights * (grad_weights - delta_rows[:, :, None])).astype(jnp.bfloat16)
    grad_query = (
        jnp.einsum("hij,jhd->ihd", grad_logits, all_keys, preferred_element_type=jnp.float32)
        * score_scale
    )
    grad_query = grad_query.astype(jnp.bfloat16).reshape(seq_rows, feature_count)
    grad_key = (
        jnp.einsum("hij,ihd->jhd", grad_logits, all_queries, preferred_element_type=jnp.float32)
        * score_scale
    )
    grad_key = grad_key.astype(jnp.bfloat16).reshape(seq_rows, feature_count)
    grad_value = jnp.einsum(
        "hij,ihd->jhd", weights_low, grad_heads, preferred_element_type=jnp.float32
    ).reshape(seq_rows, feature_count)
    gain_sum = jnp.sum(grad_value * normed, axis=0)

    grad_queries = grad_query.reshape(1, 1, seq_rows, feature_count)
    grad_keys = grad_key.reshape(1, 1, seq_rows, feature_count)
    grad_inputs = input_grads[:seq_rows].reshape(1, 1, seq_rows, feature_count)
    group_count = lax.axis_size("dp")
    gain_parts = lax.all_to_all(
        gain_sum.reshape(group_count, feature_count // group_count), "dp", 0, 0, tiled=True
    )
    grad_gains = jnp.sum(gain_parts, axis=0, keepdims=True)
    return (grad_inputs, grad_queries, grad_keys, grad_gains)


def solution(mesh):
    return jax.shard_map(
        on_device,
        mesh=mesh,
        in_specs=(
            P("pipe", "dp", None, None),
            P("pipe", "dp", None, None),
            P("pipe", "dp", None, None),
            P("dp", None, None),
            P("pipe", None),
            P(),
        ),
        out_specs=(
            P("pipe", "dp", None, None),
            P("pipe", "dp", None, None),
            P("pipe", "dp", None, None),
            P("pipe", "dp"),
        ),
        check_vma=False,
    )
```

```python
import functools
import math

import jax
import jax.numpy as jnp
from jax import lax
from jax.experimental import pallas as pl
from jax.experimental.pallas import tpu as pltpu
from jax.sharding import PartitionSpec as P

GROUPS = 8
WINDOW = 32


EPSILON = 1e-05
NEGATIVE = -1e30


def passed_along(value, axis, steps):
    count = lax.axis_size(axis)
    leading, last = (max(0, -steps), min(count, count - steps))
    return lax.ppermute(value, axis, [(source, source + steps) for source in range(leading, last)])


def rows_of(source, first_index, row_count):
    return lax.dynamic_slice_in_dim(source, first_index, row_count, 0)


def write_rows(buffer, first_index, new_rows):
    return lax.dynamic_update_slice_in_dim(buffer, new_rows, first_index, 0)


def turn_kernel(
    flags_ref,
    w_hbm, g_hbm, ig_hbm, msg_ref, loss_ref, normed_ref, inv_ref, gain_ref,
    out_ref, g_out, ig_out,
    w_v, g_v, inc_v, gn_v, sems,
    *, group_lanes, head_size, rows_here, groups, seq_rows, feature_count,
):
    chosen = flags_ref[0]
    from_loss = flags_ref[1] == 1
    active = flags_ref[2] == 1
    slot = pl.multiple_of(flags_ref[3], rows_here)
    group_heads = group_lanes // head_size
    reads = []
    for g in range(groups):
        w_copy = pltpu.make_async_copy(w_hbm.at[g, :, chosen], w_v.at[g], sems.at[0, g])
        g_copy = pltpu.make_async_copy(
            g_hbm.at[pl.ds(0, seq_rows), pl.ds(g * group_lanes, group_lanes)],
            g_v.at[g],
            sems.at[1, g],
        )
        w_copy.start()
        g_copy.start()
        reads.append((w_copy, g_copy))
    inc = jnp.where(from_loss, loss_ref[...], msg_ref[...])
    inc = jnp.where(active, inc, jnp.zeros_like(inc))
    inc_v[...] = inc
    first_row = pl.multiple_of(chosen * rows_here, rows_here)
    lane_head = lax.broadcasted_iota(jnp.int32, (rows_here, group_lanes), 1) // head_size
    total = jnp.zeros((rows_here, 1), jnp.float32)
    for g in range(groups):
        cols = slice(g * group_lanes, (g + 1) * group_lanes)
        w_copy, g_copy = reads[g]
        w_copy.wait()
        g_copy.wait()
        g_v[g, pl.ds(first_row, rows_here), :] = inc_v[:, cols]
        stacked = jnp.dot(
            w_v[g].reshape(group_heads * rows_here, seq_rows),
            g_v[g],
            preferred_element_type=jnp.float32,
        )
        value = jnp.zeros((rows_here, group_lanes), jnp.float32)
        for k in range(group_heads):
            value = value + jnp.where(
                lane_head == k, stacked[k * rows_here:(k + 1) * rows_here, :], 0.0
            )
        grad_normed = value * gain_ref[:, cols]
        gn_v[g] = grad_normed
        total = total + jnp.sum(grad_normed * normed_ref[:, cols], axis=1, keepdims=True)
    g_write = pltpu.make_async_copy(inc_v, g_out.at[pl.ds(slot, rows_here)], sems.at[2, 0])
    g_write.start()
    mean = total * (1.0 / feature_count)
    inv = inv_ref[...]
    for g in range(groups):
        cols = slice(g * group_lanes, (g + 1) * group_lanes)
        out_ref[:, cols] = (
            inc_v[:, cols].astype(jnp.float32) + inv * (gn_v[g] - normed_ref[:, cols] * mean)
        ).astype(out_ref.dtype)
    ig_write = pltpu.make_async_copy(out_ref, ig_out.at[pl.ds(slot, rows_here)], sems.at[2, 1])
    ig_write.start()
    g_write.wait()
    ig_write.wait()


def turn_call(flags, w_split, grad_buffer, input_grads, message, from_loss, normed, inverse, gain,
              *, head_size, rows_here):
    groups, group_heads, unit_count, _, seq_rows = w_split.shape
    feature_count = grad_buffer.shape[1]
    group_lanes = feature_count // groups
    kernel = functools.partial(
        turn_kernel, group_lanes=group_lanes, head_size=head_size, rows_here=rows_here,
        groups=groups, seq_rows=seq_rows, feature_count=feature_count,
    )
    grid_spec = pltpu.PrefetchScalarGridSpec(
        num_scalar_prefetch=1,
        grid=(1,),
        in_specs=[
            pl.BlockSpec(memory_space=pl.ANY),
            pl.BlockSpec(memory_space=pl.ANY),
            pl.BlockSpec(memory_space=pl.ANY),
            pl.BlockSpec((rows_here, feature_count), lambda i, f: (0, 0)),
            pl.BlockSpec((rows_here, feature_count), lambda i, f: (f[0], 0)),
            pl.BlockSpec((rows_here, feature_count), lambda i, f: (f[0], 0)),
            pl.BlockSpec((rows_here, 1), lambda i, f: (f[0], 0)),
            pl.BlockSpec((1, feature_count), lambda i, f: (0, 0)),
        ],
        out_specs=[
            pl.BlockSpec((rows_here, feature_count), lambda i, f: (0, 0)),
            pl.BlockSpec(memory_space=pl.ANY),
            pl.BlockSpec(memory_space=pl.ANY),
        ],
        scratch_shapes=[
            pltpu.VMEM((groups, group_heads, rows_here, seq_rows), jnp.bfloat16),
            pltpu.VMEM((groups, seq_rows, group_lanes), jnp.bfloat16),
            pltpu.VMEM((rows_here, feature_count), jnp.bfloat16),
            pltpu.VMEM((groups, rows_here, group_lanes), jnp.float32),
            pltpu.SemaphoreType.DMA((3, groups)),
        ],
    )
    return pl.pallas_call(
        kernel,
        grid_spec=grid_spec,
        out_shape=[
            jax.ShapeDtypeStruct((rows_here, feature_count), jnp.bfloat16),
            jax.ShapeDtypeStruct(grad_buffer.shape, grad_buffer.dtype),
            jax.ShapeDtypeStruct(input_grads.shape, input_grads.dtype),
        ],
        input_output_aliases={2: 1, 3: 2},
        compiler_params=pltpu.CompilerParams(dimension_semantics=("arbitrary",)),
    )(flags, w_split, grad_buffer, input_grads, message, from_loss, normed, inverse, gain)


def on_device(query_acts, key_acts, layer_inputs, grad_out, norm_gains, window_flags):
    section_count = lax.axis_size("pipe")
    section_index = lax.axis_index("pipe")
    seq_rows = query_acts.shape[2]
    feature_count = query_acts.shape[3]
    head_count = window_flags.shape[0]
    head_size = feature_count // head_count
    score_scale = head_size ** (-0.5)
    slopes = jnp.exp2(-(jnp.arange(head_count, dtype=jnp.float32) + 1.0) * 8.0 / head_count)
    open_heads = (window_flags == 0)[:, None, None]
    query_rows = query_acts[0, 0]
    key_rows = key_acts[0, 0]
    from_loss = grad_out[0]
    input_rows = layer_inputs[0, 0].astype(jnp.float32)
    inverse = lax.rsqrt(jnp.mean(input_rows * input_rows, axis=-1, keepdims=True) + EPSILON)
    normed = input_rows * inverse
    gain_row = norm_gains[0]
    value_rows = (normed * gain_row).astype(jnp.bfloat16)
    places = jnp.arange(seq_rows, dtype=jnp.int32)
    all_queries = query_rows.reshape(seq_rows, head_count, head_size)
    all_keys = key_rows.reshape(seq_rows, head_count, head_size)
    all_values = value_rows.reshape(seq_rows, head_count, head_size)

    distance = places[None, :] - places[:, None]
    allowed = (distance >= 0)[None, :, :] & (open_heads | (distance < WINDOW)[None, :, :])
    logits = (
        jnp.einsum("jhd,ihd->hji", all_keys, all_queries, preferred_element_type=jnp.float32)
        * score_scale
    )
    logits = logits - slopes[:, None, None] * distance.astype(jnp.float32)[None, :, :]
    masked = jnp.where(allowed, logits, NEGATIVE)
    row_top = jnp.max(masked, axis=1, keepdims=True)
    log_total = row_top + jnp.log(jnp.sum(jnp.exp(masked - row_top), axis=1, keepdims=True))
    weights = jnp.where(allowed, jnp.exp(masked - log_total), 0.0)
    weights_low = weights.astype(jnp.bfloat16)
    attended = jnp.einsum(
        "hji,jhd->ihd", weights_low, all_values, preferred_element_type=jnp.float32
    )

    unit_count = GROUPS
    rows_here = seq_rows // unit_count
    group_lanes = math.lcm(head_size, 128)
    groups = feature_count // group_lanes
    spare_rows = seq_rows + rows_here
    w_split = weights_low.reshape(
        groups, group_lanes // head_size, unit_count, rows_here, seq_rows
    )
    last_stage = (section_index == section_count - 1).astype(jnp.int32)
    gain_line = gain_row[None, :]

    def one_turn(turn_index, carried):
        message, grad_buffer, input_grads = carried
        unit_index = turn_index - (section_count - 1 - section_index)
        active = (unit_index >= 0) & (unit_index < unit_count)
        chosen = jnp.clip(unit_count - 1 - unit_index, 0, unit_count - 1)
        slot = jnp.where(active, chosen * rows_here, seq_rows)
        flags = jnp.stack([chosen, last_stage, active.astype(jnp.int32), slot])
        grad_input, grad_buffer, input_grads = turn_call(
            flags, w_split, grad_buffer, input_grads, message, from_loss, normed, inverse,
            gain_line, head_size=head_size, rows_here=rows_here,
        )
        return (passed_along(grad_input, "pipe", -1), grad_buffer, input_grads)

    initial = (
        jnp.zeros((rows_here, feature_count), jnp.bfloat16),
        jnp.zeros((spare_rows, feature_count), jnp.bfloat16),
        jnp.zeros((spare_rows, feature_count), jnp.bfloat16),
    )
    _, grad_buffer, input_grads = lax.fori_loop(
        0, unit_count + section_count - 1, one_turn, initial
    )
    grad_heads = grad_buffer[:seq_rows].reshape(seq_rows, head_count, head_size)

    delta_rows = jnp.einsum("ihd,ihd->hi", grad_heads.astype(jnp.float32), attended)
    grad_weights = jnp.einsum(
        "jhd,ihd->hji", all_values, grad_heads, preferred_element_type=jnp.float32
    )
    grad_logits = (weights * (grad_weights - delta_rows[:, None, :])).astype(jnp.bfloat16)
    grad_query = (
        jnp.einsum("hji,jhd->ihd", grad_logits, all_keys, preferred_element_type=jnp.float32)
        * score_scale
    )
    grad_query = grad_query.astype(jnp.bfloat16).reshape(seq_rows, feature_count)
    grad_key = (
        jnp.einsum("hji,ihd->jhd", grad_logits, all_queries, preferred_element_type=jnp.float32)
        * score_scale
    )
    grad_key = grad_key.astype(jnp.bfloat16).reshape(seq_rows, feature_count)
    grad_value = jnp.einsum(
        "hji,ihd->jhd", weights_low, grad_heads, preferred_element_type=jnp.float32
    ).reshape(seq_rows, feature_count)
    gain_sum = jnp.sum(grad_value * normed, axis=0)

    grad_queries = grad_query.reshape(1, 1, seq_rows, feature_count)
    grad_keys = grad_key.reshape(1, 1, seq_rows, feature_count)
    grad_inputs = input_grads[:seq_rows].reshape(1, 1, seq_rows, feature_count)
    group_count = lax.axis_size("dp")
    gain_parts = lax.all_to_all(
        gain_sum.reshape(group_count, feature_count // group_count), "dp", 0, 0, tiled=True
    )
    grad_gains = jnp.sum(gain_parts, axis=0, keepdims=True)
    return (grad_inputs, grad_queries, grad_keys, grad_gains)


def solution(mesh):
    return jax.shard_map(
        on_device,
        mesh=mesh,
        in_specs=(
            P("pipe", "dp", None, None),
            P("pipe", "dp", None, None),
            P("pipe", "dp", None, None),
            P("dp", None, None),
            P("pipe", None),
            P(),
        ),
        out_specs=(
            P("pipe", "dp", None, None),
            P("pipe", "dp", None, None),
            P("pipe", "dp", None, None),
            P("pipe", "dp"),
        ),
        check_vma=False,
    )
```

```python
import functools
import math

import jax
import jax.numpy as jnp
from jax import lax
from jax.experimental import pallas as pl
from jax.experimental.pallas import tpu as pltpu
from jax.sharding import PartitionSpec as P

GROUPS = 16
WINDOW = 32


EPSILON = 1e-05
NEGATIVE = -1e30


def passed_along(value, axis, steps):
    count = lax.axis_size(axis)
    leading, last = (max(0, -steps), min(count, count - steps))
    return lax.ppermute(value, axis, [(source, source + steps) for source in range(leading, last)])


def rows_of(source, first_index, row_count):
    return lax.dynamic_slice_in_dim(source, first_index, row_count, 0)


def write_rows(buffer, first_index, new_rows):
    return lax.dynamic_update_slice_in_dim(buffer, new_rows, first_index, 0)


def turn_kernel(
    turn_ref, stage_ref,
    w_hbm, g_hbm, ig_hbm, msg_ref, loss_ref, normed_ref, inv_ref, gain_ref,
    out_ref, g_out, ig_out,
    w_v, g_v, inc_v, gn_v, sems,
    *, group_lanes, head_size, rows_here, groups, seq_rows, feature_count, stage_count, unit_count,
):
    unit_index = turn_ref[0] - (stage_count - 1 - stage_ref[0])
    active = (unit_index >= 0) & (unit_index < unit_count)
    chosen = jnp.clip(unit_count - 1 - unit_index, 0, unit_count - 1)
    from_loss = stage_ref[0] == stage_count - 1
    slot = pl.multiple_of(jnp.where(active, chosen * rows_here, seq_rows), rows_here)
    group_heads = group_lanes // head_size
    reads = []
    for g in range(groups):
        w_copy = pltpu.make_async_copy(w_hbm.at[g, :, chosen], w_v.at[g], sems.at[0, g])
        g_copy = pltpu.make_async_copy(
            g_hbm.at[pl.ds(0, seq_rows), pl.ds(g * group_lanes, group_lanes)],
            g_v.at[g],
            sems.at[1, g],
        )
        w_copy.start()
        g_copy.start()
        reads.append((w_copy, g_copy))
    inc = jnp.where(from_loss, loss_ref[...], msg_ref[...])
    inc = jnp.where(active, inc, jnp.zeros_like(inc))
    inc_v[...] = inc
    first_row = pl.multiple_of(chosen * rows_here, rows_here)
    lane_head = lax.broadcasted_iota(jnp.int32, (rows_here, group_lanes), 1) // head_size
    total = jnp.zeros((rows_here, 1), jnp.float32)
    for g in range(groups):
        cols = slice(g * group_lanes, (g + 1) * group_lanes)
        w_copy, g_copy = reads[g]
        w_copy.wait()
        g_copy.wait()
        g_v[g, pl.ds(first_row, rows_here), :] = inc_v[:, cols]
        stacked = jnp.dot(
            w_v[g].reshape(group_heads * rows_here, seq_rows),
            g_v[g],
            preferred_element_type=jnp.float32,
        )
        value = jnp.zeros((rows_here, group_lanes), jnp.float32)
        for k in range(group_heads):
            value = value + jnp.where(
                lane_head == k, stacked[k * rows_here:(k + 1) * rows_here, :], 0.0
            )
        grad_normed = value * gain_ref[:, cols]
        gn_v[g] = grad_normed
        total = total + jnp.sum(grad_normed * normed_ref[:, cols], axis=1, keepdims=True)
    g_write = pltpu.make_async_copy(inc_v, g_out.at[pl.ds(slot, rows_here)], sems.at[2, 0])
    g_write.start()
    mean = total * (1.0 / feature_count)
    inv = inv_ref[...]
    for g in range(groups):
        cols = slice(g * group_lanes, (g + 1) * group_lanes)
        out_ref[:, cols] = (
            inc_v[:, cols].astype(jnp.float32) + inv * (gn_v[g] - normed_ref[:, cols] * mean)
        ).astype(out_ref.dtype)
    ig_write = pltpu.make_async_copy(out_ref, ig_out.at[pl.ds(slot, rows_here)], sems.at[2, 1])
    ig_write.start()
    g_write.wait()
    ig_write.wait()


def turn_call(turn, stage, w_split, grad_buffer, input_grads, message, from_loss, normed, inverse,
              gain, *, head_size, rows_here, stage_count):
    groups, group_heads, unit_count, _, seq_rows = w_split.shape
    feature_count = grad_buffer.shape[1]
    group_lanes = feature_count // groups
    kernel = functools.partial(
        turn_kernel, group_lanes=group_lanes, head_size=head_size, rows_here=rows_here,
        groups=groups, seq_rows=seq_rows, feature_count=feature_count, stage_count=stage_count,
        unit_count=unit_count,
    )

    def chunk_of(i, t, s):
        return jnp.clip(unit_count - 1 - (t[0] - (stage_count - 1 - s[0])), 0, unit_count - 1)

    grid_spec = pltpu.PrefetchScalarGridSpec(
        num_scalar_prefetch=2,
        grid=(1,),
        in_specs=[
            pl.BlockSpec(memory_space=pl.ANY),
            pl.BlockSpec(memory_space=pl.ANY),
            pl.BlockSpec(memory_space=pl.ANY),
            pl.BlockSpec((rows_here, feature_count), lambda i, t, s: (0, 0)),
            pl.BlockSpec((rows_here, feature_count), lambda i, t, s: (chunk_of(i, t, s), 0)),
            pl.BlockSpec((rows_here, feature_count), lambda i, t, s: (chunk_of(i, t, s), 0)),
            pl.BlockSpec((rows_here, 1), lambda i, t, s: (chunk_of(i, t, s), 0)),
            pl.BlockSpec((1, feature_count), lambda i, t, s: (0, 0)),
        ],
        out_specs=[
            pl.BlockSpec((rows_here, feature_count), lambda i, t, s: (0, 0)),
            pl.BlockSpec(memory_space=pl.ANY),
            pl.BlockSpec(memory_space=pl.ANY),
        ],
        scratch_shapes=[
            pltpu.VMEM((groups, group_heads, rows_here, seq_rows), jnp.bfloat16),
            pltpu.VMEM((groups, seq_rows, group_lanes), jnp.bfloat16),
            pltpu.VMEM((rows_here, feature_count), jnp.bfloat16),
            pltpu.VMEM((groups, rows_here, group_lanes), jnp.float32),
            pltpu.SemaphoreType.DMA((3, groups)),
        ],
    )
    return pl.pallas_call(
        kernel,
        grid_spec=grid_spec,
        out_shape=[
            jax.ShapeDtypeStruct((rows_here, feature_count), jnp.bfloat16),
            jax.ShapeDtypeStruct(grad_buffer.shape, grad_buffer.dtype),
            jax.ShapeDtypeStruct(input_grads.shape, input_grads.dtype),
        ],
        input_output_aliases={3: 1, 4: 2},
        compiler_params=pltpu.CompilerParams(dimension_semantics=("arbitrary",)),
    )(turn, stage, w_split, grad_buffer, input_grads, message, from_loss, normed, inverse, gain)


def on_device(query_acts, key_acts, layer_inputs, grad_out, norm_gains, window_flags):
    section_count = lax.axis_size("pipe")
    section_index = lax.axis_index("pipe")
    seq_rows = query_acts.shape[2]
    feature_count = query_acts.shape[3]
    head_count = window_flags.shape[0]
    head_size = feature_count // head_count
    score_scale = head_size ** (-0.5)
    slopes = jnp.exp2(-(jnp.arange(head_count, dtype=jnp.float32) + 1.0) * 8.0 / head_count)
    open_heads = (window_flags == 0)[:, None, None]
    query_rows = query_acts[0, 0]
    key_rows = key_acts[0, 0]
    from_loss = grad_out[0]
    input_rows = layer_inputs[0, 0].astype(jnp.float32)
    inverse = lax.rsqrt(jnp.mean(input_rows * input_rows, axis=-1, keepdims=True) + EPSILON)
    normed = input_rows * inverse
    gain_row = norm_gains[0]
    value_rows = (normed * gain_row).astype(jnp.bfloat16)
    places = jnp.arange(seq_rows, dtype=jnp.int32)
    all_queries = query_rows.reshape(seq_rows, head_count, head_size)
    all_keys = key_rows.reshape(seq_rows, head_count, head_size)
    all_values = value_rows.reshape(seq_rows, head_count, head_size)

    distance = places[None, :] - places[:, None]
    allowed = (distance >= 0)[None, :, :] & (open_heads | (distance < WINDOW)[None, :, :])
    logits = (
        jnp.einsum("jhd,ihd->hji", all_keys, all_queries, preferred_element_type=jnp.float32)
        * score_scale
    )
    logits = logits - slopes[:, None, None] * distance.astype(jnp.float32)[None, :, :]
    masked = jnp.where(allowed, logits, NEGATIVE)
    row_top = jnp.max(masked, axis=1, keepdims=True)
    log_total = row_top + jnp.log(jnp.sum(jnp.exp(masked - row_top), axis=1, keepdims=True))
    weights = jnp.where(allowed, jnp.exp(masked - log_total), 0.0)
    weights_low = weights.astype(jnp.bfloat16)
    attended = jnp.einsum(
        "hji,jhd->ihd", weights_low, all_values, preferred_element_type=jnp.float32
    )

    unit_count = GROUPS
    rows_here = seq_rows // unit_count
    group_lanes = math.lcm(head_size, 128)
    groups = feature_count // group_lanes
    spare_rows = seq_rows + rows_here
    w_split = weights_low.reshape(
        groups, group_lanes // head_size, unit_count, rows_here, seq_rows
    )
    stage = section_index.astype(jnp.int32).reshape(1)
    gain_line = gain_row[None, :]

    def one_turn(turn_index, carried):
        message, grad_buffer, input_grads = carried
        grad_input, grad_buffer, input_grads = turn_call(
            turn_index.astype(jnp.int32).reshape(1), stage, w_split, grad_buffer, input_grads,
            message, from_loss, normed, inverse, gain_line,
            head_size=head_size, rows_here=rows_here, stage_count=section_count,
        )
        return (passed_along(grad_input, "pipe", -1), grad_buffer, input_grads)

    initial = (
        jnp.zeros((rows_here, feature_count), jnp.bfloat16),
        jnp.zeros((spare_rows, feature_count), jnp.bfloat16),
        jnp.zeros((spare_rows, feature_count), jnp.bfloat16),
    )
    _, grad_buffer, input_grads = lax.fori_loop(
        0, unit_count + section_count - 1, one_turn, initial
    )
    grad_heads = grad_buffer[:seq_rows].reshape(seq_rows, head_count, head_size)

    delta_rows = jnp.einsum("ihd,ihd->hi", grad_heads.astype(jnp.float32), attended)
    grad_weights = jnp.einsum(
        "jhd,ihd->hji", all_values, grad_heads, preferred_element_type=jnp.float32
    )
    grad_logits = (weights * (grad_weights - delta_rows[:, None, :])).astype(jnp.bfloat16)
    grad_query = (
        jnp.einsum("hji,jhd->ihd", grad_logits, all_keys, preferred_element_type=jnp.float32)
        * score_scale
    )
    grad_query = grad_query.astype(jnp.bfloat16).reshape(seq_rows, feature_count)
    grad_key = (
        jnp.einsum("hji,ihd->jhd", grad_logits, all_queries, preferred_element_type=jnp.float32)
        * score_scale
    )
    grad_key = grad_key.astype(jnp.bfloat16).reshape(seq_rows, feature_count)
    grad_value = jnp.einsum(
        "hji,ihd->jhd", weights_low, grad_heads, preferred_element_type=jnp.float32
    ).reshape(seq_rows, feature_count)
    gain_sum = jnp.sum(grad_value * normed, axis=0)

    grad_queries = grad_query.reshape(1, 1, seq_rows, feature_count)
    grad_keys = grad_key.reshape(1, 1, seq_rows, feature_count)
    grad_inputs = input_grads[:seq_rows].reshape(1, 1, seq_rows, feature_count)
    group_count = lax.axis_size("dp")
    gain_parts = lax.all_to_all(
        gain_sum.reshape(group_count, feature_count // group_count), "dp", 0, 0, tiled=True
    )
    grad_gains = jnp.sum(gain_parts, axis=0, keepdims=True)
    return (grad_inputs, grad_queries, grad_keys, grad_gains)


def solution(mesh):
    return jax.shard_map(
        on_device,
        mesh=mesh,
        in_specs=(
            P("pipe", "dp", None, None),
            P("pipe", "dp", None, None),
            P("pipe", "dp", None, None),
            P("dp", None, None),
            P("pipe", None),
            P(),
        ),
        out_specs=(
            P("pipe", "dp", None, None),
            P("pipe", "dp", None, None),
            P("pipe", "dp", None, None),
            P("pipe", "dp"),
        ),
        check_vma=False,
    )
```

```python
import functools
import math

import jax
import jax.numpy as jnp
from jax import lax
from jax.experimental import pallas as pl
from jax.experimental.pallas import tpu as pltpu
from jax.sharding import PartitionSpec as P

GROUPS = 8
WINDOW = 32


EPSILON = 1e-05
NEGATIVE = -1e30


def passed_along(value, axis, steps):
    count = lax.axis_size(axis)
    leading, last = (max(0, -steps), min(count, count - steps))
    return lax.ppermute(value, axis, [(source, source + steps) for source in range(leading, last)])


def rows_of(source, first_index, row_count):
    return lax.dynamic_slice_in_dim(source, first_index, row_count, 0)


def write_rows(buffer, first_index, new_rows):
    return lax.dynamic_update_slice_in_dim(buffer, new_rows, first_index, 0)


def turn_kernel(
    turn_ref, stage_ref,
    w_hbm, g_hbm, ig_hbm, msg_ref, loss_ref, normed_ref, inv_ref, gain_ref,
    out_ref, g_out, ig_out,
    w_v, gn_v, normed_v, loss_v, sems,
    *, group_lanes, head_size, rows_here, groups, seq_rows, feature_count, stage_count, unit_count,
):
    unit_index = turn_ref[0] - (stage_count - 1 - stage_ref[0])
    active = (unit_index >= 0) & (unit_index < unit_count)
    chosen = jnp.clip(unit_count - 1 - unit_index, 0, unit_count - 1)
    from_loss = stage_ref[0] == stage_count - 1
    slot = pl.multiple_of(jnp.where(active, chosen * rows_here, seq_rows), rows_here)
    group_heads = group_lanes // head_size
    w_copies = []
    for g in range(groups):
        w_copy = pltpu.make_async_copy(w_hbm.at[g, :, chosen], w_v.at[g], sems.at[0, g])
        w_copy.start()
        w_copies.append(w_copy)
    first_row = pl.multiple_of(chosen * rows_here, rows_here)
    normed_copy = pltpu.make_async_copy(
        normed_ref.at[pl.ds(first_row, rows_here)], normed_v, sems.at[1, 0]
    )
    loss_copy = pltpu.make_async_copy(
        loss_ref.at[pl.ds(first_row, rows_here)], loss_v, sems.at[1, 1]
    )
    normed_copy.start()
    loss_copy.start()
    loss_copy.wait()
    inc = jnp.where(from_loss, loss_v[...], msg_ref[...])
    inc = jnp.where(active, inc, jnp.zeros_like(inc))
    g_out[pl.ds(slot, rows_here), :] = inc
    lane_head = lax.broadcasted_iota(jnp.int32, (rows_here, group_lanes), 1) // head_size
    total = jnp.zeros((rows_here, 1), jnp.float32)
    normed_copy.wait()
    for g in range(groups):
        cols = slice(g * group_lanes, (g + 1) * group_lanes)
        w_copies[g].wait()
        stacked = jnp.dot(
            w_v[g].reshape(group_heads * rows_here, seq_rows),
            g_out[pl.ds(0, seq_rows), cols],
            preferred_element_type=jnp.float32,
        )
        value = jnp.zeros((rows_here, group_lanes), jnp.float32)
        for k in range(group_heads):
            value = value + jnp.where(
                lane_head == k, stacked[k * rows_here:(k + 1) * rows_here, :], 0.0
            )
        grad_normed = value * gain_ref[:, cols]
        gn_v[g] = grad_normed
        total = total + jnp.sum(grad_normed * normed_v[:, cols], axis=1, keepdims=True)
    mean = total * (1.0 / feature_count)
    inv = inv_ref[...]
    for g in range(groups):
        cols = slice(g * group_lanes, (g + 1) * group_lanes)
        out_ref[:, cols] = (
            inc[:, cols].astype(jnp.float32) + inv * (gn_v[g] - normed_v[:, cols] * mean)
        ).astype(out_ref.dtype)
    ig_write = pltpu.make_async_copy(out_ref, ig_out.at[pl.ds(slot, rows_here)], sems.at[2, 0])
    ig_write.start()
    ig_write.wait()


def turn_call(turn, stage, w_split, grad_buffer, input_grads, message, from_loss, normed, inverse,
              gain, *, head_size, rows_here, stage_count):
    groups, group_heads, unit_count, _, seq_rows = w_split.shape
    feature_count = grad_buffer.shape[1]
    group_lanes = feature_count // groups
    kernel = functools.partial(
        turn_kernel, group_lanes=group_lanes, head_size=head_size, rows_here=rows_here,
        groups=groups, seq_rows=seq_rows, feature_count=feature_count, stage_count=stage_count,
        unit_count=unit_count,
    )

    def chunk_of(i, t, s):
        return jnp.clip(unit_count - 1 - (t[0] - (stage_count - 1 - s[0])), 0, unit_count - 1)

    grid_spec = pltpu.PrefetchScalarGridSpec(
        num_scalar_prefetch=2,
        grid=(1,),
        in_specs=[
            pl.BlockSpec(memory_space=pl.ANY),
            pl.BlockSpec(memory_space=pltpu.VMEM),
            pl.BlockSpec(memory_space=pl.ANY),
            pl.BlockSpec((rows_here, feature_count), lambda i, t, s: (0, 0)),
            pl.BlockSpec(memory_space=pl.ANY),
            pl.BlockSpec(memory_space=pl.ANY),
            pl.BlockSpec((rows_here, 1), lambda i, t, s: (chunk_of(i, t, s), 0)),
            pl.BlockSpec((1, feature_count), lambda i, t, s: (0, 0)),
        ],
        out_specs=[
            pl.BlockSpec((rows_here, feature_count), lambda i, t, s: (0, 0)),
            pl.BlockSpec(memory_space=pltpu.VMEM),
            pl.BlockSpec(memory_space=pl.ANY),
        ],
        scratch_shapes=[
            pltpu.VMEM((groups, group_heads, rows_here, seq_rows), jnp.bfloat16),
            pltpu.VMEM((groups, rows_here, group_lanes), jnp.float32),
            pltpu.VMEM((rows_here, feature_count), jnp.float32),
            pltpu.VMEM((rows_here, feature_count), jnp.bfloat16),
            pltpu.SemaphoreType.DMA((3, groups)),
        ],
    )
    return pl.pallas_call(
        kernel,
        grid_spec=grid_spec,
        out_shape=[
            jax.ShapeDtypeStruct((rows_here, feature_count), jnp.bfloat16),
            jax.ShapeDtypeStruct(grad_buffer.shape, grad_buffer.dtype),
            jax.ShapeDtypeStruct(input_grads.shape, input_grads.dtype),
        ],
        input_output_aliases={3: 1, 4: 2},
        compiler_params=pltpu.CompilerParams(dimension_semantics=("arbitrary",)),
    )(turn, stage, w_split, grad_buffer, input_grads, message, from_loss, normed, inverse, gain)


def on_device(query_acts, key_acts, layer_inputs, grad_out, norm_gains, window_flags):
    section_count = lax.axis_size("pipe")
    section_index = lax.axis_index("pipe")
    seq_rows = query_acts.shape[2]
    feature_count = query_acts.shape[3]
    head_count = window_flags.shape[0]
    head_size = feature_count // head_count
    score_scale = head_size ** (-0.5)
    slopes = jnp.exp2(-(jnp.arange(head_count, dtype=jnp.float32) + 1.0) * 8.0 / head_count)
    open_heads = (window_flags == 0)[:, None, None]
    query_rows = query_acts[0, 0]
    key_rows = key_acts[0, 0]
    from_loss = grad_out[0]
    input_rows = layer_inputs[0, 0].astype(jnp.float32)
    inverse = lax.rsqrt(jnp.mean(input_rows * input_rows, axis=-1, keepdims=True) + EPSILON)
    normed = input_rows * inverse
    gain_row = norm_gains[0]
    value_rows = (normed * gain_row).astype(jnp.bfloat16)
    places = jnp.arange(seq_rows, dtype=jnp.int32)
    all_queries = query_rows.reshape(seq_rows, head_count, head_size)
    all_keys = key_rows.reshape(seq_rows, head_count, head_size)
    all_values = value_rows.reshape(seq_rows, head_count, head_size)

    distance = places[None, :] - places[:, None]
    allowed = (distance >= 0)[None, :, :] & (open_heads | (distance < WINDOW)[None, :, :])
    logits = (
        jnp.einsum("jhd,ihd->hji", all_keys, all_queries, preferred_element_type=jnp.float32)
        * score_scale
    )
    logits = logits - slopes[:, None, None] * distance.astype(jnp.float32)[None, :, :]
    masked = jnp.where(allowed, logits, NEGATIVE)
    row_top = jnp.max(masked, axis=1, keepdims=True)
    log_total = row_top + jnp.log(jnp.sum(jnp.exp(masked - row_top), axis=1, keepdims=True))
    weights = jnp.where(allowed, jnp.exp(masked - log_total), 0.0)
    weights_low = weights.astype(jnp.bfloat16)
    attended = jnp.einsum(
        "hji,jhd->ihd", weights_low, all_values, preferred_element_type=jnp.float32
    )

    unit_count = GROUPS
    rows_here = seq_rows // unit_count
    group_lanes = math.lcm(head_size, 128)
    groups = feature_count // group_lanes
    spare_rows = seq_rows + rows_here
    w_split = weights_low.reshape(
        groups, group_lanes // head_size, unit_count, rows_here, seq_rows
    )
    stage = section_index.astype(jnp.int32).reshape(1)
    gain_line = gain_row[None, :]

    def one_turn(turn_index, carried):
        message, grad_buffer, input_grads = carried
        grad_input, grad_buffer, input_grads = turn_call(
            turn_index.astype(jnp.int32).reshape(1), stage, w_split, grad_buffer, input_grads,
            message, from_loss, normed, inverse, gain_line,
            head_size=head_size, rows_here=rows_here, stage_count=section_count,
        )
        return (passed_along(grad_input, "pipe", -1), grad_buffer, input_grads)

    initial = (
        jnp.zeros((rows_here, feature_count), jnp.bfloat16),
        jnp.zeros((spare_rows, feature_count), jnp.bfloat16),
        jnp.zeros((spare_rows, feature_count), jnp.bfloat16),
    )
    _, grad_buffer, input_grads = lax.fori_loop(
        0, unit_count + section_count - 1, one_turn, initial
    )
    grad_heads = grad_buffer[:seq_rows].reshape(seq_rows, head_count, head_size)

    delta_rows = jnp.einsum("ihd,ihd->hi", grad_heads.astype(jnp.float32), attended)
    grad_weights = jnp.einsum(
        "jhd,ihd->hji", all_values, grad_heads, preferred_element_type=jnp.float32
    )
    grad_logits = (weights * (grad_weights - delta_rows[:, None, :])).astype(jnp.bfloat16)
    grad_query = (
        jnp.einsum("hji,jhd->ihd", grad_logits, all_keys, preferred_element_type=jnp.float32)
        * score_scale
    )
    grad_query = grad_query.astype(jnp.bfloat16).reshape(seq_rows, feature_count)
    grad_key = (
        jnp.einsum("hji,ihd->jhd", grad_logits, all_queries, preferred_element_type=jnp.float32)
        * score_scale
    )
    grad_key = grad_key.astype(jnp.bfloat16).reshape(seq_rows, feature_count)
    grad_value = jnp.einsum(
        "hji,ihd->jhd", weights_low, grad_heads, preferred_element_type=jnp.float32
    ).reshape(seq_rows, feature_count)
    gain_sum = jnp.sum(grad_value * normed, axis=0)

    grad_queries = grad_query.reshape(1, 1, seq_rows, feature_count)
    grad_keys = grad_key.reshape(1, 1, seq_rows, feature_count)
    grad_inputs = input_grads[:seq_rows].reshape(1, 1, seq_rows, feature_count)
    group_count = lax.axis_size("dp")
    gain_parts = lax.all_to_all(
        gain_sum.reshape(group_count, feature_count // group_count), "dp", 0, 0, tiled=True
    )
    grad_gains = jnp.sum(gain_parts, axis=0, keepdims=True)
    return (grad_inputs, grad_queries, grad_keys, grad_gains)


def solution(mesh):
    return jax.shard_map(
        on_device,
        mesh=mesh,
        in_specs=(
            P("pipe", "dp", None, None),
            P("pipe", "dp", None, None),
            P("pipe", "dp", None, None),
            P("dp", None, None),
            P("pipe", None),
            P(),
        ),
        out_specs=(
            P("pipe", "dp", None, None),
            P("pipe", "dp", None, None),
            P("pipe", "dp", None, None),
            P("pipe", "dp"),
        ),
        check_vma=False,
    )
```

```python
import functools
import math

import jax
import jax.numpy as jnp
from jax import lax
from jax.experimental import pallas as pl
from jax.experimental.pallas import tpu as pltpu
from jax.sharding import PartitionSpec as P

GROUPS = 8
WINDOW = 32


EPSILON = 1e-05
NEGATIVE = -1e30


def passed_along(value, axis, steps):
    count = lax.axis_size(axis)
    leading, last = (max(0, -steps), min(count, count - steps))
    return lax.ppermute(value, axis, [(source, source + steps) for source in range(leading, last)])


def rows_of(source, first_index, row_count):
    return lax.dynamic_slice_in_dim(source, first_index, row_count, 0)


def write_rows(buffer, first_index, new_rows):
    return lax.dynamic_update_slice_in_dim(buffer, new_rows, first_index, 0)


def turn_kernel(
    turn_ref, stage_ref,
    w_hbm, g_hbm, ig_hbm, msg_ref, loss_ref, normed_ref, inv_ref, gain_ref,
    out_ref, g_out, ig_out,
    w_v, gn_v, normed_v, loss_v, sems,
    *, group_lanes, head_size, rows_here, groups, seq_rows, feature_count, stage_count, unit_count,
):
    unit_index = turn_ref[0] - (stage_count - 1 - stage_ref[0])
    active = (unit_index >= 0) & (unit_index < unit_count)
    chosen = jnp.clip(unit_count - 1 - unit_index, 0, unit_count - 1)
    from_loss = stage_ref[0] == stage_count - 1
    slot = pl.multiple_of(jnp.where(active, chosen * rows_here, seq_rows), rows_here)
    group_heads = group_lanes // head_size
    w_copies = []
    for g in range(groups):
        w_copy = pltpu.make_async_copy(w_hbm.at[g, :, chosen], w_v.at[g], sems.at[0, g])
        w_copy.start()
        w_copies.append(w_copy)
    first_row = pl.multiple_of(chosen * rows_here, rows_here)
    normed_copy = pltpu.make_async_copy(
        normed_ref.at[pl.ds(first_row, rows_here)], normed_v, sems.at[1, 0]
    )
    loss_copy = pltpu.make_async_copy(
        loss_ref.at[pl.ds(first_row, rows_here)], loss_v, sems.at[1, 1]
    )
    normed_copy.start()
    loss_copy.start()
    loss_copy.wait()
    inc = jnp.where(from_loss, loss_v[...], msg_ref[...])
    inc = jnp.where(active, inc, jnp.zeros_like(inc))
    g_out[pl.ds(slot, rows_here), :] = inc
    lane_head = lax.broadcasted_iota(jnp.int32, (rows_here, group_lanes), 1) // head_size
    total = jnp.zeros((rows_here, 1), jnp.float32)
    normed_copy.wait()
    for g in range(groups):
        cols = slice(g * group_lanes, (g + 1) * group_lanes)
        w_copies[g].wait()
        stacked = jnp.dot(
            w_v[g].reshape(group_heads * rows_here, seq_rows),
            g_out[pl.ds(0, seq_rows), cols],
            preferred_element_type=jnp.float32,
        )
        value = jnp.zeros((rows_here, group_lanes), jnp.float32)
        for k in range(group_heads):
            value = value + jnp.where(
                lane_head == k, stacked[k * rows_here:(k + 1) * rows_here, :], 0.0
            )
        grad_normed = value * gain_ref[:, cols]
        gn_v[g] = grad_normed
        total = total + jnp.sum(grad_normed * normed_v[:, cols], axis=1, keepdims=True)
    mean = total * (1.0 / feature_count)
    inv = inv_ref[pl.ds(first_row, rows_here), :]
    for g in range(groups):
        cols = slice(g * group_lanes, (g + 1) * group_lanes)
        out_ref[:, cols] = (
            inc[:, cols].astype(jnp.float32) + inv * (gn_v[g] - normed_v[:, cols] * mean)
        ).astype(out_ref.dtype)
    ig_write = pltpu.make_async_copy(out_ref, ig_out.at[pl.ds(slot, rows_here)], sems.at[2, 0])
    ig_write.start()
    ig_write.wait()


def turn_call(turn, stage, w_split, grad_buffer, input_grads, message, from_loss, normed, inverse,
              gain, *, head_size, rows_here, stage_count):
    groups, group_heads, unit_count, _, seq_rows = w_split.shape
    feature_count = grad_buffer.shape[1]
    group_lanes = feature_count // groups
    kernel = functools.partial(
        turn_kernel, group_lanes=group_lanes, head_size=head_size, rows_here=rows_here,
        groups=groups, seq_rows=seq_rows, feature_count=feature_count, stage_count=stage_count,
        unit_count=unit_count,
    )

    def chunk_of(i, t, s):
        return jnp.clip(unit_count - 1 - (t[0] - (stage_count - 1 - s[0])), 0, unit_count - 1)

    grid_spec = pltpu.PrefetchScalarGridSpec(
        num_scalar_prefetch=2,
        grid=(1,),
        in_specs=[
            pl.BlockSpec(memory_space=pl.ANY),
            pl.BlockSpec(memory_space=pltpu.VMEM),
            pl.BlockSpec(memory_space=pl.ANY),
            pl.BlockSpec(memory_space=pltpu.VMEM),
            pl.BlockSpec(memory_space=pl.ANY),
            pl.BlockSpec(memory_space=pl.ANY),
            pl.BlockSpec(memory_space=pltpu.VMEM),
            pl.BlockSpec(memory_space=pltpu.VMEM),
        ],
        out_specs=[
            pl.BlockSpec(memory_space=pltpu.VMEM),
            pl.BlockSpec(memory_space=pltpu.VMEM),
            pl.BlockSpec(memory_space=pl.ANY),
        ],
        scratch_shapes=[
            pltpu.VMEM((groups, group_heads, rows_here, seq_rows), jnp.bfloat16),
            pltpu.VMEM((groups, rows_here, group_lanes), jnp.float32),
            pltpu.VMEM((rows_here, feature_count), jnp.float32),
            pltpu.VMEM((rows_here, feature_count), jnp.bfloat16),
            pltpu.SemaphoreType.DMA((3, groups)),
        ],
    )
    return pl.pallas_call(
        kernel,
        grid_spec=grid_spec,
        out_shape=[
            jax.ShapeDtypeStruct((rows_here, feature_count), jnp.bfloat16),
            jax.ShapeDtypeStruct(grad_buffer.shape, grad_buffer.dtype),
            jax.ShapeDtypeStruct(input_grads.shape, input_grads.dtype),
        ],
        input_output_aliases={3: 1, 4: 2},
        compiler_params=pltpu.CompilerParams(dimension_semantics=("arbitrary",)),
    )(turn, stage, w_split, grad_buffer, input_grads, message, from_loss, normed, inverse, gain)


def on_device(query_acts, key_acts, layer_inputs, grad_out, norm_gains, window_flags):
    section_count = lax.axis_size("pipe")
    section_index = lax.axis_index("pipe")
    seq_rows = query_acts.shape[2]
    feature_count = query_acts.shape[3]
    head_count = window_flags.shape[0]
    head_size = feature_count // head_count
    score_scale = head_size ** (-0.5)
    slopes = jnp.exp2(-(jnp.arange(head_count, dtype=jnp.float32) + 1.0) * 8.0 / head_count)
    open_heads = (window_flags == 0)[:, None, None]
    query_rows = query_acts[0, 0]
    key_rows = key_acts[0, 0]
    from_loss = grad_out[0]
    input_rows = layer_inputs[0, 0].astype(jnp.float32)
    inverse = lax.rsqrt(jnp.mean(input_rows * input_rows, axis=-1, keepdims=True) + EPSILON)
    normed = input_rows * inverse
    gain_row = norm_gains[0]
    value_rows = (normed * gain_row).astype(jnp.bfloat16)
    places = jnp.arange(seq_rows, dtype=jnp.int32)
    all_queries = query_rows.reshape(seq_rows, head_count, head_size)
    all_keys = key_rows.reshape(seq_rows, head_count, head_size)
    all_values = value_rows.reshape(seq_rows, head_count, head_size)

    distance = places[None, :] - places[:, None]
    allowed = (distance >= 0)[None, :, :] & (open_heads | (distance < WINDOW)[None, :, :])
    logits = (
        jnp.einsum("jhd,ihd->hji", all_keys, all_queries, preferred_element_type=jnp.float32)
        * score_scale
    )
    logits = logits - slopes[:, None, None] * distance.astype(jnp.float32)[None, :, :]
    masked = jnp.where(allowed, logits, NEGATIVE)
    row_top = jnp.max(masked, axis=1, keepdims=True)
    log_total = row_top + jnp.log(jnp.sum(jnp.exp(masked - row_top), axis=1, keepdims=True))
    weights = jnp.where(allowed, jnp.exp(masked - log_total), 0.0)
    weights_low = weights.astype(jnp.bfloat16)
    attended = jnp.einsum(
        "hji,jhd->ihd", weights_low, all_values, preferred_element_type=jnp.float32
    )

    unit_count = GROUPS
    rows_here = seq_rows // unit_count
    group_lanes = math.lcm(head_size, 128)
    groups = feature_count // group_lanes
    spare_rows = seq_rows + rows_here
    w_split = weights_low.reshape(
        groups, group_lanes // head_size, unit_count, rows_here, seq_rows
    )
    stage = section_index.astype(jnp.int32).reshape(1)
    gain_line = gain_row[None, :]

    def one_turn(turn_index, carried):
        message, grad_buffer, input_grads = carried
        grad_input, grad_buffer, input_grads = turn_call(
            turn_index.astype(jnp.int32).reshape(1), stage, w_split, grad_buffer, input_grads,
            message, from_loss, normed, inverse, gain_line,
            head_size=head_size, rows_here=rows_here, stage_count=section_count,
        )
        return (passed_along(grad_input, "pipe", -1), grad_buffer, input_grads)

    initial = (
        jnp.zeros((rows_here, feature_count), jnp.bfloat16),
        jnp.zeros((spare_rows, feature_count), jnp.bfloat16),
        jnp.zeros((spare_rows, feature_count), jnp.bfloat16),
    )
    _, grad_buffer, input_grads = lax.fori_loop(
        0, unit_count + section_count - 1, one_turn, initial
    )
    grad_heads = grad_buffer[:seq_rows].reshape(seq_rows, head_count, head_size)

    delta_rows = jnp.einsum("ihd,ihd->hi", grad_heads.astype(jnp.float32), attended)
    grad_weights = jnp.einsum(
        "jhd,ihd->hji", all_values, grad_heads, preferred_element_type=jnp.float32
    )
    grad_logits = (weights * (grad_weights - delta_rows[:, None, :])).astype(jnp.bfloat16)
    grad_query = (
        jnp.einsum("hji,jhd->ihd", grad_logits, all_keys, preferred_element_type=jnp.float32)
        * score_scale
    )
    grad_query = grad_query.astype(jnp.bfloat16).reshape(seq_rows, feature_count)
    grad_key = (
        jnp.einsum("hji,ihd->jhd", grad_logits, all_queries, preferred_element_type=jnp.float32)
        * score_scale
    )
    grad_key = grad_key.astype(jnp.bfloat16).reshape(seq_rows, feature_count)
    grad_value = jnp.einsum(
        "hji,ihd->jhd", weights_low, grad_heads, preferred_element_type=jnp.float32
    ).reshape(seq_rows, feature_count)
    gain_sum = jnp.sum(grad_value * normed, axis=0)

    grad_queries = grad_query.reshape(1, 1, seq_rows, feature_count)
    grad_keys = grad_key.reshape(1, 1, seq_rows, feature_count)
    grad_inputs = input_grads[:seq_rows].reshape(1, 1, seq_rows, feature_count)
    group_count = lax.axis_size("dp")
    gain_parts = lax.all_to_all(
        gain_sum.reshape(group_count, feature_count // group_count), "dp", 0, 0, tiled=True
    )
    grad_gains = jnp.sum(gain_parts, axis=0, keepdims=True)
    return (grad_inputs, grad_queries, grad_keys, grad_gains)


def solution(mesh):
    return jax.shard_map(
        on_device,
        mesh=mesh,
        in_specs=(
            P("pipe", "dp", None, None),
            P("pipe", "dp", None, None),
            P("pipe", "dp", None, None),
            P("dp", None, None),
            P("pipe", None),
            P(),
        ),
        out_specs=(
            P("pipe", "dp", None, None),
            P("pipe", "dp", None, None),
            P("pipe", "dp", None, None),
            P("pipe", "dp"),
        ),
        check_vma=False,
    )
```

```python
import functools
import math

import jax
import jax.numpy as jnp
from jax import lax
from jax.experimental import pallas as pl
from jax.experimental.pallas import tpu as pltpu
from jax.sharding import PartitionSpec as P

GROUPS = 8
WINDOW = 32


EPSILON = 1e-05
NEGATIVE = -1e30


def passed_along(value, axis, steps):
    count = lax.axis_size(axis)
    leading, last = (max(0, -steps), min(count, count - steps))
    return lax.ppermute(value, axis, [(source, source + steps) for source in range(leading, last)])


def rows_of(source, first_index, row_count):
    return lax.dynamic_slice_in_dim(source, first_index, row_count, 0)


def write_rows(buffer, first_index, new_rows):
    return lax.dynamic_update_slice_in_dim(buffer, new_rows, first_index, 0)


def turn_kernel(
    turn_ref, stage_ref,
    w_hbm, g_hbm, ig_hbm, sum_in, msg_ref, loss_ref, normed_ref, inv_ref, gain_ref,
    out_ref, g_out, ig_out, sum_out,
    w_v, gn_v, normed_v, loss_v, sems,
    *, group_lanes, head_size, rows_here, groups, seq_rows, feature_count, stage_count, unit_count,
):
    unit_index = turn_ref[0] - (stage_count - 1 - stage_ref[0])
    active = (unit_index >= 0) & (unit_index < unit_count)
    chosen = jnp.clip(unit_count - 1 - unit_index, 0, unit_count - 1)
    from_loss = stage_ref[0] == stage_count - 1
    slot = pl.multiple_of(jnp.where(active, chosen * rows_here, seq_rows), rows_here)
    group_heads = group_lanes // head_size
    w_copies = []
    for g in range(groups):
        w_copy = pltpu.make_async_copy(w_hbm.at[g, :, chosen], w_v.at[g], sems.at[0, g])
        w_copy.start()
        w_copies.append(w_copy)
    first_row = pl.multiple_of(chosen * rows_here, rows_here)
    normed_copy = pltpu.make_async_copy(
        normed_ref.at[pl.ds(first_row, rows_here)], normed_v, sems.at[1, 0]
    )
    loss_copy = pltpu.make_async_copy(
        loss_ref.at[pl.ds(first_row, rows_here)], loss_v, sems.at[1, 1]
    )
    normed_copy.start()
    loss_copy.start()
    loss_copy.wait()
    inc = jnp.where(from_loss, loss_v[...], msg_ref[...])
    inc = jnp.where(active, inc, jnp.zeros_like(inc))
    g_out[pl.ds(slot, rows_here), :] = inc
    lane_head = lax.broadcasted_iota(jnp.int32, (rows_here, group_lanes), 1) // head_size
    total = jnp.zeros((rows_here, 1), jnp.float32)
    normed_copy.wait()
    for g in range(groups):
        cols = slice(g * group_lanes, (g + 1) * group_lanes)
        w_copies[g].wait()
        stacked = jnp.dot(
            w_v[g].reshape(group_heads * rows_here, seq_rows),
            g_out[pl.ds(0, seq_rows), cols],
            preferred_element_type=jnp.float32,
        )
        value = jnp.zeros((rows_here, group_lanes), jnp.float32)
        for k in range(group_heads):
            value = value + jnp.where(
                lane_head == k, stacked[k * rows_here:(k + 1) * rows_here, :], 0.0
            )
        gain_part = jnp.sum(value * normed_v[:, cols], axis=0, keepdims=True)
        sum_out[:, cols] = sum_out[:, cols] + jnp.where(active, gain_part, 0.0)
        grad_normed = value * gain_ref[:, cols]
        gn_v[g] = grad_normed
        total = total + jnp.sum(grad_normed * normed_v[:, cols], axis=1, keepdims=True)
    mean = total * (1.0 / feature_count)
    inv = inv_ref[...]
    for g in range(groups):
        cols = slice(g * group_lanes, (g + 1) * group_lanes)
        out_ref[:, cols] = (
            inc[:, cols].astype(jnp.float32) + inv * (gn_v[g] - normed_v[:, cols] * mean)
        ).astype(out_ref.dtype)
    ig_write = pltpu.make_async_copy(out_ref, ig_out.at[pl.ds(slot, rows_here)], sems.at[2, 0])
    ig_write.start()
    ig_write.wait()


def turn_call(turn, stage, w_split, grad_buffer, input_grads, gain_sum, message, from_loss, normed,
              inverse, gain, *, head_size, rows_here, stage_count):
    groups, group_heads, unit_count, _, seq_rows = w_split.shape
    feature_count = grad_buffer.shape[1]
    group_lanes = feature_count // groups
    kernel = functools.partial(
        turn_kernel, group_lanes=group_lanes, head_size=head_size, rows_here=rows_here,
        groups=groups, seq_rows=seq_rows, feature_count=feature_count, stage_count=stage_count,
        unit_count=unit_count,
    )

    def chunk_of(i, t, s):
        return jnp.clip(unit_count - 1 - (t[0] - (stage_count - 1 - s[0])), 0, unit_count - 1)

    grid_spec = pltpu.PrefetchScalarGridSpec(
        num_scalar_prefetch=2,
        grid=(1,),
        in_specs=[
            pl.BlockSpec(memory_space=pl.ANY),
            pl.BlockSpec(memory_space=pltpu.VMEM),
            pl.BlockSpec(memory_space=pl.ANY),
            pl.BlockSpec(memory_space=pltpu.VMEM),
            pl.BlockSpec((rows_here, feature_count), lambda i, t, s: (0, 0)),
            pl.BlockSpec(memory_space=pl.ANY),
            pl.BlockSpec(memory_space=pl.ANY),
            pl.BlockSpec((rows_here, 1), lambda i, t, s: (chunk_of(i, t, s), 0)),
            pl.BlockSpec((1, feature_count), lambda i, t, s: (0, 0)),
        ],
        out_specs=[
            pl.BlockSpec((rows_here, feature_count), lambda i, t, s: (0, 0)),
            pl.BlockSpec(memory_space=pltpu.VMEM),
            pl.BlockSpec(memory_space=pl.ANY),
            pl.BlockSpec(memory_space=pltpu.VMEM),
        ],
        scratch_shapes=[
            pltpu.VMEM((groups, group_heads, rows_here, seq_rows), jnp.bfloat16),
            pltpu.VMEM((groups, rows_here, group_lanes), jnp.float32),
            pltpu.VMEM((rows_here, feature_count), jnp.float32),
            pltpu.VMEM((rows_here, feature_count), jnp.bfloat16),
            pltpu.SemaphoreType.DMA((3, groups)),
        ],
    )
    return pl.pallas_call(
        kernel,
        grid_spec=grid_spec,
        out_shape=[
            jax.ShapeDtypeStruct((rows_here, feature_count), jnp.bfloat16),
            jax.ShapeDtypeStruct(grad_buffer.shape, grad_buffer.dtype),
            jax.ShapeDtypeStruct(input_grads.shape, input_grads.dtype),
            jax.ShapeDtypeStruct(gain_sum.shape, gain_sum.dtype),
        ],
        input_output_aliases={3: 1, 4: 2, 5: 3},
        compiler_params=pltpu.CompilerParams(dimension_semantics=("arbitrary",)),
    )(turn, stage, w_split, grad_buffer, input_grads, gain_sum, message, from_loss, normed, inverse,
      gain)


def on_device(query_acts, key_acts, layer_inputs, grad_out, norm_gains, window_flags):
    section_count = lax.axis_size("pipe")
    section_index = lax.axis_index("pipe")
    seq_rows = query_acts.shape[2]
    feature_count = query_acts.shape[3]
    head_count = window_flags.shape[0]
    head_size = feature_count // head_count
    score_scale = head_size ** (-0.5)
    slopes = jnp.exp2(-(jnp.arange(head_count, dtype=jnp.float32) + 1.0) * 8.0 / head_count)
    open_heads = (window_flags == 0)[:, None, None]
    query_rows = query_acts[0, 0]
    key_rows = key_acts[0, 0]
    from_loss = grad_out[0]
    input_rows = layer_inputs[0, 0].astype(jnp.float32)
    inverse = lax.rsqrt(jnp.mean(input_rows * input_rows, axis=-1, keepdims=True) + EPSILON)
    normed = input_rows * inverse
    gain_row = norm_gains[0]
    value_rows = (normed * gain_row).astype(jnp.bfloat16)
    places = jnp.arange(seq_rows, dtype=jnp.int32)
    all_queries = query_rows.reshape(seq_rows, head_count, head_size)
    all_keys = key_rows.reshape(seq_rows, head_count, head_size)
    all_values = value_rows.reshape(seq_rows, head_count, head_size)

    distance = places[None, :] - places[:, None]
    allowed = (distance >= 0)[None, :, :] & (open_heads | (distance < WINDOW)[None, :, :])
    logits = (
        jnp.einsum("jhd,ihd->hji", all_keys, all_queries, preferred_element_type=jnp.float32)
        * score_scale
    )
    logits = logits - slopes[:, None, None] * distance.astype(jnp.float32)[None, :, :]
    masked = jnp.where(allowed, logits, NEGATIVE)
    row_top = jnp.max(masked, axis=1, keepdims=True)
    log_total = row_top + jnp.log(jnp.sum(jnp.exp(masked - row_top), axis=1, keepdims=True))
    weights = jnp.where(allowed, jnp.exp(masked - log_total), 0.0)
    weights_low = weights.astype(jnp.bfloat16)
    attended = jnp.einsum(
        "hji,jhd->ihd", weights_low, all_values, preferred_element_type=jnp.float32
    )

    unit_count = GROUPS
    rows_here = seq_rows // unit_count
    group_lanes = math.lcm(head_size, 128)
    groups = feature_count // group_lanes
    spare_rows = seq_rows + rows_here
    w_split = weights_low.reshape(
        groups, group_lanes // head_size, unit_count, rows_here, seq_rows
    )
    stage = section_index.astype(jnp.int32).reshape(1)
    gain_line = gain_row[None, :]

    def one_turn(turn_index, carried):
        message, grad_buffer, input_grads, gain_total = carried
        grad_input, grad_buffer, input_grads, gain_total = turn_call(
            turn_index.astype(jnp.int32).reshape(1), stage, w_split, grad_buffer, input_grads,
            gain_total, message, from_loss, normed, inverse, gain_line,
            head_size=head_size, rows_here=rows_here, stage_count=section_count,
        )
        return (passed_along(grad_input, "pipe", -1), grad_buffer, input_grads, gain_total)

    initial = (
        jnp.zeros((rows_here, feature_count), jnp.bfloat16),
        jnp.zeros((spare_rows, feature_count), jnp.bfloat16),
        jnp.zeros((spare_rows, feature_count), jnp.bfloat16),
        jnp.zeros((1, feature_count), jnp.float32),
    )
    _, grad_buffer, input_grads, gain_total = lax.fori_loop(
        0, unit_count + section_count - 1, one_turn, initial
    )
    grad_heads = grad_buffer[:seq_rows].reshape(seq_rows, head_count, head_size)

    delta_rows = jnp.einsum("ihd,ihd->hi", grad_heads.astype(jnp.float32), attended)
    grad_weights = jnp.einsum(
        "jhd,ihd->hji", all_values, grad_heads, preferred_element_type=jnp.float32
    )
    grad_logits = (weights * (grad_weights - delta_rows[:, None, :])).astype(jnp.bfloat16)
    grad_query = (
        jnp.einsum("hji,jhd->ihd", grad_logits, all_keys, preferred_element_type=jnp.float32)
        * score_scale
    )
    grad_query = grad_query.astype(jnp.bfloat16).reshape(seq_rows, feature_count)
    grad_key = (
        jnp.einsum("hji,ihd->jhd", grad_logits, all_queries, preferred_element_type=jnp.float32)
        * score_scale
    )
    grad_key = grad_key.astype(jnp.bfloat16).reshape(seq_rows, feature_count)
    gain_sum = gain_total[0]

    grad_queries = grad_query.reshape(1, 1, seq_rows, feature_count)
    grad_keys = grad_key.reshape(1, 1, seq_rows, feature_count)
    grad_inputs = input_grads[:seq_rows].reshape(1, 1, seq_rows, feature_count)
    group_count = lax.axis_size("dp")
    gain_parts = lax.all_to_all(
        gain_sum.reshape(group_count, feature_count // group_count), "dp", 0, 0, tiled=True
    )
    grad_gains = jnp.sum(gain_parts, axis=0, keepdims=True)
    return (grad_inputs, grad_queries, grad_keys, grad_gains)


def solution(mesh):
    return jax.shard_map(
        on_device,
        mesh=mesh,
        in_specs=(
            P("pipe", "dp", None, None),
            P("pipe", "dp", None, None),
            P("pipe", "dp", None, None),
            P("dp", None, None),
            P("pipe", None),
            P(),
        ),
        out_specs=(
            P("pipe", "dp", None, None),
            P("pipe", "dp", None, None),
            P("pipe", "dp", None, None),
            P("pipe", "dp"),
        ),
        check_vma=False,
    )
```

```python
import functools
import math

import jax
import jax.numpy as jnp
from jax import lax
from jax.experimental import pallas as pl
from jax.experimental.pallas import tpu as pltpu
from jax.sharding import PartitionSpec as P

GROUPS = 16
WINDOW = 32


EPSILON = 1e-05
NEGATIVE = -1e30


def passed_along(value, axis, steps):
    count = lax.axis_size(axis)
    leading, last = (max(0, -steps), min(count, count - steps))
    return lax.ppermute(value, axis, [(source, source + steps) for source in range(leading, last)])


def rows_of(source, first_index, row_count):
    return lax.dynamic_slice_in_dim(source, first_index, row_count, 0)


def write_rows(buffer, first_index, new_rows):
    return lax.dynamic_update_slice_in_dim(buffer, new_rows, first_index, 0)


def turn_kernel(
    turn_ref, stage_ref,
    w_hbm, g_hbm, ig_hbm, msg_ref, loss_ref, normed_ref, inv_ref, gain_ref,
    out_ref, g_out, ig_out,
    w_v, gn_v, normed_v, loss_v, sems,
    *, group_lanes, head_size, rows_here, groups, seq_rows, feature_count, stage_count, unit_count,
):
    unit_index = turn_ref[0] - (stage_count - 1 - stage_ref[0])
    active = (unit_index >= 0) & (unit_index < unit_count)
    chosen = jnp.clip(unit_count - 1 - unit_index, 0, unit_count - 1)
    from_loss = stage_ref[0] == stage_count - 1
    slot = pl.multiple_of(jnp.where(active, chosen * rows_here, seq_rows), rows_here)
    group_heads = group_lanes // head_size
    w_copies = []
    for g in range(groups):
        w_copy = pltpu.make_async_copy(w_hbm.at[g, :, chosen], w_v.at[g], sems.at[0, g])
        w_copy.start()
        w_copies.append(w_copy)
    first_row = pl.multiple_of(chosen * rows_here, rows_here)
    normed_copy = pltpu.make_async_copy(
        normed_ref.at[pl.ds(first_row, rows_here)], normed_v, sems.at[1, 0]
    )
    loss_copy = pltpu.make_async_copy(
        loss_ref.at[pl.ds(first_row, rows_here)], loss_v, sems.at[1, 1]
    )
    normed_copy.start()
    loss_copy.start()
    loss_copy.wait()
    inc = jnp.where(from_loss, loss_v[...], msg_ref[...])
    inc = jnp.where(active, inc, jnp.zeros_like(inc))
    g_out[pl.ds(slot, rows_here), :] = inc
    lane_head = lax.broadcasted_iota(jnp.int32, (rows_here, group_lanes), 1) // head_size
    total = jnp.zeros((rows_here, 1), jnp.float32)
    normed_copy.wait()
    for g in range(groups):
        cols = slice(g * group_lanes, (g + 1) * group_lanes)
        w_copies[g].wait()
        stacked = jnp.dot(
            w_v[g].reshape(group_heads * rows_here, seq_rows),
            g_out[pl.ds(0, seq_rows), cols],
            preferred_element_type=jnp.float32,
        )
        value = jnp.zeros((rows_here, group_lanes), jnp.float32)
        for k in range(group_heads):
            value = value + jnp.where(
                lane_head == k, stacked[k * rows_here:(k + 1) * rows_here, :], 0.0
            )
        grad_normed = value * gain_ref[:, cols]
        gn_v[g] = grad_normed
        total = total + jnp.sum(grad_normed * normed_v[:, cols], axis=1, keepdims=True)
    mean = total * (1.0 / feature_count)
    inv = inv_ref[...]
    for g in range(groups):
        cols = slice(g * group_lanes, (g + 1) * group_lanes)
        out_ref[:, cols] = (
            inc[:, cols].astype(jnp.float32) + inv * (gn_v[g] - normed_v[:, cols] * mean)
        ).astype(out_ref.dtype)
    ig_write = pltpu.make_async_copy(out_ref, ig_out.at[pl.ds(slot, rows_here)], sems.at[2, 0])
    ig_write.start()
    ig_write.wait()


def turn_call(turn, stage, w_split, grad_buffer, input_grads, message, from_loss, normed, inverse,
              gain, *, head_size, rows_here, stage_count):
    groups, group_heads, unit_count, _, seq_rows = w_split.shape
    feature_count = grad_buffer.shape[1]
    group_lanes = feature_count // groups
    kernel = functools.partial(
        turn_kernel, group_lanes=group_lanes, head_size=head_size, rows_here=rows_here,
        groups=groups, seq_rows=seq_rows, feature_count=feature_count, stage_count=stage_count,
        unit_count=unit_count,
    )

    def chunk_of(i, t, s):
        return jnp.clip(unit_count - 1 - (t[0] - (stage_count - 1 - s[0])), 0, unit_count - 1)

    grid_spec = pltpu.PrefetchScalarGridSpec(
        num_scalar_prefetch=2,
        grid=(1,),
        in_specs=[
            pl.BlockSpec(memory_space=pl.ANY),
            pl.BlockSpec(memory_space=pltpu.VMEM),
            pl.BlockSpec(memory_space=pl.ANY),
            pl.BlockSpec((rows_here, feature_count), lambda i, t, s: (0, 0)),
            pl.BlockSpec(memory_space=pl.ANY),
            pl.BlockSpec(memory_space=pl.ANY),
            pl.BlockSpec((rows_here, 1), lambda i, t, s: (chunk_of(i, t, s), 0)),
            pl.BlockSpec((1, feature_count), lambda i, t, s: (0, 0)),
        ],
        out_specs=[
            pl.BlockSpec((rows_here, feature_count), lambda i, t, s: (0, 0)),
            pl.BlockSpec(memory_space=pltpu.VMEM),
            pl.BlockSpec(memory_space=pl.ANY),
        ],
        scratch_shapes=[
            pltpu.VMEM((groups, group_heads, rows_here, seq_rows), jnp.bfloat16),
            pltpu.VMEM((groups, rows_here, group_lanes), jnp.float32),
            pltpu.VMEM((rows_here, feature_count), jnp.float32),
            pltpu.VMEM((rows_here, feature_count), jnp.bfloat16),
            pltpu.SemaphoreType.DMA((3, groups)),
        ],
    )
    return pl.pallas_call(
        kernel,
        grid_spec=grid_spec,
        out_shape=[
            jax.ShapeDtypeStruct((rows_here, feature_count), jnp.bfloat16),
            jax.ShapeDtypeStruct(grad_buffer.shape, grad_buffer.dtype),
            jax.ShapeDtypeStruct(input_grads.shape, input_grads.dtype),
        ],
        input_output_aliases={3: 1, 4: 2},
        compiler_params=pltpu.CompilerParams(dimension_semantics=("arbitrary",)),
    )(turn, stage, w_split, grad_buffer, input_grads, message, from_loss, normed, inverse, gain)


def on_device(query_acts, key_acts, layer_inputs, grad_out, norm_gains, window_flags):
    section_count = lax.axis_size("pipe")
    section_index = lax.axis_index("pipe")
    seq_rows = query_acts.shape[2]
    feature_count = query_acts.shape[3]
    head_count = window_flags.shape[0]
    head_size = feature_count // head_count
    score_scale = head_size ** (-0.5)
    slopes = jnp.exp2(-(jnp.arange(head_count, dtype=jnp.float32) + 1.0) * 8.0 / head_count)
    open_heads = (window_flags == 0)[:, None, None]
    query_rows = query_acts[0, 0]
    key_rows = key_acts[0, 0]
    from_loss = grad_out[0]
    input_rows = layer_inputs[0, 0].astype(jnp.float32)
    inverse = lax.rsqrt(jnp.mean(input_rows * input_rows, axis=-1, keepdims=True) + EPSILON)
    normed = input_rows * inverse
    gain_row = norm_gains[0]
    value_rows = (normed * gain_row).astype(jnp.bfloat16)
    places = jnp.arange(seq_rows, dtype=jnp.int32)
    all_queries = query_rows.reshape(seq_rows, head_count, head_size)
    all_keys = key_rows.reshape(seq_rows, head_count, head_size)
    all_values = value_rows.reshape(seq_rows, head_count, head_size)

    distance = places[None, :] - places[:, None]
    allowed = (distance >= 0)[None, :, :] & (open_heads | (distance < WINDOW)[None, :, :])
    logits = (
        jnp.einsum("jhd,ihd->hji", all_keys, all_queries, preferred_element_type=jnp.float32)
        * score_scale
    )
    logits = logits - slopes[:, None, None] * distance.astype(jnp.float32)[None, :, :]
    masked = jnp.where(allowed, logits, NEGATIVE)
    row_top = jnp.max(masked, axis=1, keepdims=True)
    log_total = row_top + jnp.log(jnp.sum(jnp.exp(masked - row_top), axis=1, keepdims=True))
    weights = jnp.where(allowed, jnp.exp(masked - log_total), 0.0)
    weights_low = weights.astype(jnp.bfloat16)
    attended = jnp.einsum(
        "hji,jhd->ihd", weights_low, all_values, preferred_element_type=jnp.float32
    )

    unit_count = GROUPS
    rows_here = seq_rows // unit_count
    group_lanes = math.lcm(head_size, 128)
    groups = feature_count // group_lanes
    spare_rows = seq_rows + rows_here
    w_split = weights_low.reshape(
        groups, group_lanes // head_size, unit_count, rows_here, seq_rows
    )
    stage = section_index.astype(jnp.int32).reshape(1)
    gain_line = gain_row[None, :]

    def one_turn(turn_index, carried):
        message, grad_buffer, input_grads = carried
        grad_input, grad_buffer, input_grads = turn_call(
            turn_index.astype(jnp.int32).reshape(1), stage, w_split, grad_buffer, input_grads,
            message, from_loss, normed, inverse, gain_line,
            head_size=head_size, rows_here=rows_here, stage_count=section_count,
        )
        return (passed_along(grad_input, "pipe", -1), grad_buffer, input_grads)

    initial = (
        jnp.zeros((rows_here, feature_count), jnp.bfloat16),
        jnp.zeros((spare_rows, feature_count), jnp.bfloat16),
        jnp.zeros((spare_rows, feature_count), jnp.bfloat16),
    )
    _, grad_buffer, input_grads = lax.fori_loop(
        0, unit_count + section_count - 1, one_turn, initial
    )
    grad_heads = grad_buffer[:seq_rows].reshape(seq_rows, head_count, head_size)

    delta_rows = jnp.einsum("ihd,ihd->hi", grad_heads.astype(jnp.float32), attended)
    grad_weights = jnp.einsum(
        "jhd,ihd->hji", all_values, grad_heads, preferred_element_type=jnp.float32
    )
    grad_logits = (weights * (grad_weights - delta_rows[:, None, :])).astype(jnp.bfloat16)
    grad_query = (
        jnp.einsum("hji,jhd->ihd", grad_logits, all_keys, preferred_element_type=jnp.float32)
        * score_scale
    )
    grad_query = grad_query.astype(jnp.bfloat16).reshape(seq_rows, feature_count)
    grad_key = (
        jnp.einsum("hji,ihd->jhd", grad_logits, all_queries, preferred_element_type=jnp.float32)
        * score_scale
    )
    grad_key = grad_key.astype(jnp.bfloat16).reshape(seq_rows, feature_count)
    grad_value = jnp.einsum(
        "hji,ihd->jhd", weights_low, grad_heads, preferred_element_type=jnp.float32
    ).reshape(seq_rows, feature_count)
    gain_sum = jnp.sum(grad_value * normed, axis=0)

    grad_queries = grad_query.reshape(1, 1, seq_rows, feature_count)
    grad_keys = grad_key.reshape(1, 1, seq_rows, feature_count)
    grad_inputs = input_grads[:seq_rows].reshape(1, 1, seq_rows, feature_count)
    group_count = lax.axis_size("dp")
    gain_parts = lax.all_to_all(
        gain_sum.reshape(group_count, feature_count // group_count), "dp", 0, 0, tiled=True
    )
    grad_gains = jnp.sum(gain_parts, axis=0, keepdims=True)
    return (grad_inputs, grad_queries, grad_keys, grad_gains)


def solution(mesh):
    return jax.shard_map(
        on_device,
        mesh=mesh,
        in_specs=(
            P("pipe", "dp", None, None),
            P("pipe", "dp", None, None),
            P("pipe", "dp", None, None),
            P("dp", None, None),
            P("pipe", None),
            P(),
        ),
        out_specs=(
            P("pipe", "dp", None, None),
            P("pipe", "dp", None, None),
            P("pipe", "dp", None, None),
            P("pipe", "dp"),
        ),
        check_vma=False,
    )
```

```python
import functools
import math

import jax
import jax.numpy as jnp
from jax import lax
from jax.experimental import pallas as pl
from jax.experimental.pallas import tpu as pltpu
from jax.sharding import PartitionSpec as P

GROUPS = 8
WINDOW = 32


EPSILON = 1e-05
NEGATIVE = -1e30


def passed_along(value, axis, steps):
    count = lax.axis_size(axis)
    leading, last = (max(0, -steps), min(count, count - steps))
    return lax.ppermute(value, axis, [(source, source + steps) for source in range(leading, last)])


def rows_of(source, first_index, row_count):
    return lax.dynamic_slice_in_dim(source, first_index, row_count, 0)


def write_rows(buffer, first_index, new_rows):
    return lax.dynamic_update_slice_in_dim(buffer, new_rows, first_index, 0)


def turn_kernel(
    turn_ref, stage_ref,
    w_hbm, g_hbm, ig_hbm, msg_ref, loss_ref, normed_ref, inv_ref, gain_ref,
    out_ref, g_out, ig_out,
    w_v, gn_v, normed_v, loss_v, sems,
    *, group_lanes, head_size, rows_here, groups, seq_rows, feature_count, stage_count, unit_count,
):
    unit_index = turn_ref[0] - (stage_count - 1 - stage_ref[0])
    active = (unit_index >= 0) & (unit_index < unit_count)
    chosen = jnp.clip(unit_count - 1 - unit_index, 0, unit_count - 1)
    from_loss = stage_ref[0] == stage_count - 1
    slot = pl.multiple_of(jnp.where(active, chosen * rows_here, seq_rows), rows_here)
    group_heads = group_lanes // head_size
    w_copies = []
    for g in range(groups):
        w_copy = pltpu.make_async_copy(w_hbm.at[g, :, chosen], w_v.at[g], sems.at[0, g])
        w_copy.start()
        w_copies.append(w_copy)
    first_row = pl.multiple_of(chosen * rows_here, rows_here)
    normed_copy = pltpu.make_async_copy(
        normed_ref.at[pl.ds(first_row, rows_here)], normed_v, sems.at[1, 0]
    )
    loss_copy = pltpu.make_async_copy(
        loss_ref.at[pl.ds(first_row, rows_here)], loss_v, sems.at[1, 1]
    )
    normed_copy.start()
    loss_copy.start()
    loss_copy.wait()
    inc = jnp.where(from_loss, loss_v[...], msg_ref[...])
    inc = jnp.where(active, inc, jnp.zeros_like(inc))
    g_out[pl.ds(slot, rows_here), :] = inc
    lane_head = lax.broadcasted_iota(jnp.int32, (rows_here, group_lanes), 1) // head_size
    total = jnp.zeros((rows_here, 1), jnp.float32)
    normed_copy.wait()
    for g in range(groups):
        cols = slice(g * group_lanes, (g + 1) * group_lanes)
        w_copies[g].wait()
        group_rows = g_out[pl.ds(0, seq_rows), cols]
        value = jnp.zeros((rows_here, group_lanes), jnp.float32)
        for k in range(group_heads):
            head_part = jnp.dot(w_v[g, k], group_rows, preferred_element_type=jnp.float32)
            value = value + jnp.where(lane_head == k, head_part, 0.0)
        grad_normed = value * gain_ref[:, cols]
        gn_v[g] = grad_normed
        total = total + jnp.sum(grad_normed * normed_v[:, cols], axis=1, keepdims=True)
    mean = total * (1.0 / feature_count)
    inv = inv_ref[...]
    for g in range(groups):
        cols = slice(g * group_lanes, (g + 1) * group_lanes)
        out_ref[:, cols] = (
            inc[:, cols].astype(jnp.float32) + inv * (gn_v[g] - normed_v[:, cols] * mean)
        ).astype(out_ref.dtype)
    ig_write = pltpu.make_async_copy(out_ref, ig_out.at[pl.ds(slot, rows_here)], sems.at[2, 0])
    ig_write.start()
    ig_write.wait()


def turn_call(turn, stage, w_split, grad_buffer, input_grads, message, from_loss, normed, inverse,
              gain, *, head_size, rows_here, stage_count):
    groups, group_heads, unit_count, _, seq_rows = w_split.shape
    feature_count = grad_buffer.shape[1]
    group_lanes = feature_count // groups
    kernel = functools.partial(
        turn_kernel, group_lanes=group_lanes, head_size=head_size, rows_here=rows_here,
        groups=groups, seq_rows=seq_rows, feature_count=feature_count, stage_count=stage_count,
        unit_count=unit_count,
    )

    def chunk_of(i, t, s):
        return jnp.clip(unit_count - 1 - (t[0] - (stage_count - 1 - s[0])), 0, unit_count - 1)

    grid_spec = pltpu.PrefetchScalarGridSpec(
        num_scalar_prefetch=2,
        grid=(1,),
        in_specs=[
            pl.BlockSpec(memory_space=pl.ANY),
            pl.BlockSpec(memory_space=pltpu.VMEM),
            pl.BlockSpec(memory_space=pl.ANY),
            pl.BlockSpec((rows_here, feature_count), lambda i, t, s: (0, 0)),
            pl.BlockSpec(memory_space=pl.ANY),
            pl.BlockSpec(memory_space=pl.ANY),
            pl.BlockSpec((rows_here, 1), lambda i, t, s: (chunk_of(i, t, s), 0)),
            pl.BlockSpec((1, feature_count), lambda i, t, s: (0, 0)),
        ],
        out_specs=[
            pl.BlockSpec((rows_here, feature_count), lambda i, t, s: (0, 0)),
            pl.BlockSpec(memory_space=pltpu.VMEM),
            pl.BlockSpec(memory_space=pl.ANY),
        ],
        scratch_shapes=[
            pltpu.VMEM((groups, group_heads, rows_here, seq_rows), jnp.bfloat16),
            pltpu.VMEM((groups, rows_here, group_lanes), jnp.float32),
            pltpu.VMEM((rows_here, feature_count), jnp.float32),
            pltpu.VMEM((rows_here, feature_count), jnp.bfloat16),
            pltpu.SemaphoreType.DMA((3, groups)),
        ],
    )
    return pl.pallas_call(
        kernel,
        grid_spec=grid_spec,
        out_shape=[
            jax.ShapeDtypeStruct((rows_here, feature_count), jnp.bfloat16),
            jax.ShapeDtypeStruct(grad_buffer.shape, grad_buffer.dtype),
            jax.ShapeDtypeStruct(input_grads.shape, input_grads.dtype),
        ],
        input_output_aliases={3: 1, 4: 2},
        compiler_params=pltpu.CompilerParams(dimension_semantics=("arbitrary",)),
    )(turn, stage, w_split, grad_buffer, input_grads, message, from_loss, normed, inverse, gain)


def on_device(query_acts, key_acts, layer_inputs, grad_out, norm_gains, window_flags):
    section_count = lax.axis_size("pipe")
    section_index = lax.axis_index("pipe")
    seq_rows = query_acts.shape[2]
    feature_count = query_acts.shape[3]
    head_count = window_flags.shape[0]
    head_size = feature_count // head_count
    score_scale = head_size ** (-0.5)
    slopes = jnp.exp2(-(jnp.arange(head_count, dtype=jnp.float32) + 1.0) * 8.0 / head_count)
    open_heads = (window_flags == 0)[:, None, None]
    query_rows = query_acts[0, 0]
    key_rows = key_acts[0, 0]
    from_loss = grad_out[0]
    input_rows = layer_inputs[0, 0].astype(jnp.float32)
    inverse = lax.rsqrt(jnp.mean(input_rows * input_rows, axis=-1, keepdims=True) + EPSILON)
    normed = input_rows * inverse
    gain_row = norm_gains[0]
    value_rows = (normed * gain_row).astype(jnp.bfloat16)
    places = jnp.arange(seq_rows, dtype=jnp.int32)
    all_queries = query_rows.reshape(seq_rows, head_count, head_size)
    all_keys = key_rows.reshape(seq_rows, head_count, head_size)
    all_values = value_rows.reshape(seq_rows, head_count, head_size)

    distance = places[None, :] - places[:, None]
    allowed = (distance >= 0)[None, :, :] & (open_heads | (distance < WINDOW)[None, :, :])
    logits = (
        jnp.einsum("jhd,ihd->hji", all_keys, all_queries, preferred_element_type=jnp.float32)
        * score_scale
    )
    logits = logits - slopes[:, None, None] * distance.astype(jnp.float32)[None, :, :]
    masked = jnp.where(allowed, logits, NEGATIVE)
    row_top = jnp.max(masked, axis=1, keepdims=True)
    log_total = row_top + jnp.log(jnp.sum(jnp.exp(masked - row_top), axis=1, keepdims=True))
    weights = jnp.where(allowed, jnp.exp(masked - log_total), 0.0)
    weights_low = weights.astype(jnp.bfloat16)
    attended = jnp.einsum(
        "hji,jhd->ihd", weights_low, all_values, preferred_element_type=jnp.float32
    )

    unit_count = GROUPS
    rows_here = seq_rows // unit_count
    group_lanes = math.lcm(head_size, 128)
    groups = feature_count // group_lanes
    spare_rows = seq_rows + rows_here
    w_split = weights_low.reshape(
        groups, group_lanes // head_size, unit_count, rows_here, seq_rows
    )
    stage = section_index.astype(jnp.int32).reshape(1)
    gain_line = gain_row[None, :]

    def one_turn(turn_index, carried):
        message, grad_buffer, input_grads = carried
        grad_input, grad_buffer, input_grads = turn_call(
            turn_index.astype(jnp.int32).reshape(1), stage, w_split, grad_buffer, input_grads,
            message, from_loss, normed, inverse, gain_line,
            head_size=head_size, rows_here=rows_here, stage_count=section_count,
        )
        return (passed_along(grad_input, "pipe", -1), grad_buffer, input_grads)

    initial = (
        jnp.zeros((rows_here, feature_count), jnp.bfloat16),
        jnp.zeros((spare_rows, feature_count), jnp.bfloat16),
        jnp.zeros((spare_rows, feature_count), jnp.bfloat16),
    )
    _, grad_buffer, input_grads = lax.fori_loop(
        0, unit_count + section_count - 1, one_turn, initial
    )
    grad_heads = grad_buffer[:seq_rows].reshape(seq_rows, head_count, head_size)

    delta_rows = jnp.einsum("ihd,ihd->hi", grad_heads.astype(jnp.float32), attended)
    grad_weights = jnp.einsum(
        "jhd,ihd->hji", all_values, grad_heads, preferred_element_type=jnp.float32
    )
    grad_logits = (weights * (grad_weights - delta_rows[:, None, :])).astype(jnp.bfloat16)
    grad_query = (
        jnp.einsum("hji,jhd->ihd", grad_logits, all_keys, preferred_element_type=jnp.float32)
        * score_scale
    )
    grad_query = grad_query.astype(jnp.bfloat16).reshape(seq_rows, feature_count)
    grad_key = (
        jnp.einsum("hji,ihd->jhd", grad_logits, all_queries, preferred_element_type=jnp.float32)
        * score_scale
    )
    grad_key = grad_key.astype(jnp.bfloat16).reshape(seq_rows, feature_count)
    grad_value = jnp.einsum(
        "hji,ihd->jhd", weights_low, grad_heads, preferred_element_type=jnp.float32
    ).reshape(seq_rows, feature_count)
    gain_sum = jnp.sum(grad_value * normed, axis=0)

    grad_queries = grad_query.reshape(1, 1, seq_rows, feature_count)
    grad_keys = grad_key.reshape(1, 1, seq_rows, feature_count)
    grad_inputs = input_grads[:seq_rows].reshape(1, 1, seq_rows, feature_count)
    group_count = lax.axis_size("dp")
    gain_parts = lax.all_to_all(
        gain_sum.reshape(group_count, feature_count // group_count), "dp", 0, 0, tiled=True
    )
    grad_gains = jnp.sum(gain_parts, axis=0, keepdims=True)
    return (grad_inputs, grad_queries, grad_keys, grad_gains)


def solution(mesh):
    return jax.shard_map(
        on_device,
        mesh=mesh,
        in_specs=(
            P("pipe", "dp", None, None),
            P("pipe", "dp", None, None),
            P("pipe", "dp", None, None),
            P("dp", None, None),
            P("pipe", None),
            P(),
        ),
        out_specs=(
            P("pipe", "dp", None, None),
            P("pipe", "dp", None, None),
            P("pipe", "dp", None, None),
            P("pipe", "dp"),
        ),
        check_vma=False,
    )
```
